32 devices in a mesh: dp: 16 (over z, x, core), tensor: 2 (over y).
Axes of the slice: x: 2, y: 2, z: 4, core: 2. Of those that a mesh axis runs over, the one named last changes fastest.
Arguments:
- tokens: bfloat16 [16384, 1024], P('dp'), may hold values from -6 to 6
- cotangent: bfloat16 [16384, 1024], P('dp'), may hold values from -6 to 6
- lengths: int32 [16, 8], P('dp'), may hold values from 0 to 1024, as said below
- norm_gain: float32 [1024], replicated, may hold values from 0.5 to 1.5
- query_weight: bfloat16 [1024, 512], P(None, 'tensor'), may hold values from -0.1875 to 0.1875
- key_weight: bfloat16 [1024, 128], P(None, 'tensor'), may hold values from -0.1875 to 0.1875
- value_weight: bfloat16 [1024, 128], P(None, 'tensor'), may hold values from -0.1875 to 0.1875
- attn_out_weight: bfloat16 [512, 1024], P('tensor'), may hold values from -4 to 4
- z_weight: bfloat16 [1024, 1536], P(None, 'tensor'), may hold values from -0.1875 to 0.1875
- x_weight: bfloat16 [1024, 1536], P(None, 'tensor'), may hold values from -0.1875 to 0.1875
- bc_weight: bfloat16 [1024, 256], replicated, may hold values from -0.1875 to 0.1875
- dt_weight: bfloat16 [1024, 24], P(None, 'tensor'), may hold values from -0.09375 to 0.09375
- conv_x: bfloat16 [4, 1536], P(None, 'tensor'), may hold values from -3 to 3
- conv_x_bias: bfloat16 [1536], P('tensor'), may hold values from -3 to 3
- conv_bc: bfloat16 [4, 256], replicated, may hold values from -3 to 3
- conv_bc_bias: bfloat16 [256], replicated, may hold values from -3 to 3
- dt_bias: float32 [24], P('tensor'), may hold values from -6 to -2
- a_log: float32 [24], P('tensor'), may hold values from 0 to 2.7
- skip_gain: float32 [24], P('tensor'), may hold values from 0.5 to 2
- mixer_gain: float32 [1536], P('tensor'), may hold values from 0.5 to 1.5
- mamba_out_weight: bfloat16 [1536, 1024], P('tensor'), may hold values from -0.15625 to 0.15625
- ffn_gain: float32 [1024], replicated, may hold values from 0.5 to 1.5
- gate_weight: bfloat16 [1024, 2048], P(None, 'tensor'), may hold values from -0.1875 to 0.1875
- up_weight: bfloat16 [1024, 2048], P(None, 'tensor'), may hold values from -0.1875 to 0.1875
- down_weight: bfloat16 [2048, 1024], P('tensor'), may hold values from -0.125 to 0.125
Outputs:
- block_output: bfloat16 [16384, 1024], P('dp')
- tokens_grad: bfloat16 [16384, 1024], P('dp')
- norm_gain_grad: float32 [1024], replicated
- query_weight_grad: float32 [1024, 512], P('dp', 'tensor')
- key_weight_grad: float32 [1024, 128], P('dp', 'tensor')
- value_weight_grad: float32 [1024, 128], P('dp', 'tensor')
- attn_out_weight_grad: float32 [512, 1024], P('tensor', 'dp')
- z_weight_grad: float32 [1024, 1536], P('dp', 'tensor')
- x_weight_grad: float32 [1024, 1536], P('dp', 'tensor')
- bc_weight_grad: float32 [1024, 256], P('dp')
- dt_weight_grad: float32 [1024, 24], P('dp', 'tensor')
- conv_x_grad: float32 [4, 1536], P(None, 'tensor')
- conv_x_bias_grad: float32 [1536], P('tensor')
- conv_bc_grad: float32 [4, 256], replicated
- conv_bc_bias_grad: float32 [256], replicated
- dt_bias_grad: float32 [24], P('tensor')
- a_log_grad: float32 [24], P('tensor')
- skip_gain_grad: float32 [24], P('tensor')
- mixer_gain_grad: float32 [1536], P('tensor')
- mamba_out_weight_grad: float32 [1536, 1024], P('tensor', 'dp')
- ffn_gain_grad: float32 [1024], replicated
- gate_weight_grad: float32 [1024, 2048], P('dp', 'tensor')
- up_weight_grad: float32 [1024, 2048], P('dp', 'tensor')
- down_weight_grad: float32 [2048, 1024], P('tensor', 'dp')
The draws below stay inside these ranges and needn't reach their ends.
Inputs may be any that keep to these rules, and one draw needn't show every extreme that they name: In each row the nonzero lengths come first; ceil(length / 128) summed over a row is at most 8; some entry equals 1024.
All inputs are finite; a program needn't handle non-finite values.
Results may differ from the reference program's by a relative error of at most 0.015.
Values sent between devices are 32-bit elements; how exact they have to be, the bound alone decides.
No kernel may reach another device: no remote copies, remote signals or barrier semaphores. Data moves between devices by JAX's collectives and lax.ppermute only.
A program may use at most 192 MiB of HBM per device.

```python
import jax
import jax.numpy as jnp
from jax import lax

D = 1024
SSM_HEADS = 24
SSM_HEAD_DIM = 64
STATE = 128
CONV_WIDTH = 4
QUERY_HEADS = 8
KV_HEADS = 2
HEAD_DIM = 64
FF = 2048
BLOCK = 128
LONGEST = 1024
BLOCKS = 8
ROWS = 1024
TOKENS = 16384
N_DP = 16


def draw_lengths(key, part):
    most_blocks = LONGEST // BLOCK
    count_key, pad_key, used_key, pick_key = jax.random.split(key, 4)
    counts = jax.random.randint(count_key, (N_DP, BLOCKS), 1, most_blocks + 1)
    padding = jax.random.randint(pad_key, (N_DP, BLOCKS), 0, BLOCK)
    budget = jax.random.randint(used_key, (N_DP, 1), BLOCKS // 2, BLOCKS + 1)
    chosen = jax.random.randint(pick_key, (), 0, N_DP)
    row_ids = jnp.arange(N_DP)[:, None]
    column_ids = jnp.arange(BLOCKS)[None, :]
    is_chosen = row_ids == chosen
    leading = is_chosen & (column_ids == 0)
    counts = jnp.where(leading, most_blocks, counts)
    padding = jnp.where(leading, 0, padding)
    budget = jnp.where(is_chosen, BLOCKS, budget)
    before = jnp.cumsum(counts, axis=1) - counts
    granted = jnp.clip(budget - before, 0, counts)
    result = jnp.where(granted > 0, granted * BLOCK - padding, 0)
    return result.astype(jnp.int32)


def shard_levels(rng, shape, cuts, smallest, high):
    level = 1.0
    for dim, blocks in cuts:
        steps = jax.random.uniform(jax.random.fold_in(jax.random.fold_in(rng, 6), dim), (blocks,), jnp.float32, smallest / len(cuts), high / len(cuts))
        level = level * jnp.repeat(jnp.exp(steps), shape[dim] // blocks).reshape((-1,) + (1,) * (len(shape) - 1 - dim))
    return level


def bell_draw(key, extent, width, limit, shards=(), kind=jnp.bfloat16):
    values = width * jax.random.normal(key, extent, jnp.float32)
    if shards:
        values = values * shard_levels(key, extent, shards, -0.22, 0.18)
    return jnp.clip(values, -limit, limit).astype(kind)


def setup_inputs(seed: int = 0) -> dict:
    splits = jax.random.split(jax.random.key(seed), 26)
    return {
        "tokens": bell_draw(splits[0], (TOKENS, D), 1.0, 6.0, ((0, 16),)),
        "cotangent": bell_draw(splits[1], (TOKENS, D), 1.0, 6.0, ((0, 16),)),
        "lengths": draw_lengths(jax.random.fold_in(splits[25], 71), 0),
        "norm_gain": jnp.clip(1.0 + 0.1 * jax.random.normal(splits[3], (D,), jnp.float32), 0.5, 1.5),
        "query_weight": bell_draw(splits[4], (D, QUERY_HEADS * HEAD_DIM), D ** -0.5, 0.1875, ((1, 2),)),
        "key_weight": bell_draw(splits[5], (D, KV_HEADS * HEAD_DIM), D ** -0.5, 0.1875, ((1, 2),)),
        "value_weight": bell_draw(splits[6], (D, KV_HEADS * HEAD_DIM), D ** -0.5, 0.1875, ((1, 2),)),
        "attn_out_weight": bell_draw(splits[7], (QUERY_HEADS * HEAD_DIM, D), (max(1, QUERY_HEADS * HEAD_DIM // 256)) ** -0.5, 4.0, ((0, 2),)),
        "z_weight": bell_draw(splits[8], (D, SSM_HEADS * SSM_HEAD_DIM), D ** -0.5, 0.1875, ((1, 2),)),
        "x_weight": bell_draw(splits[9], (D, SSM_HEADS * SSM_HEAD_DIM), D ** -0.5, 0.1875, ((1, 2),)),
        "bc_weight": bell_draw(splits[10], (D, 2 * STATE), D ** -0.5, 0.1875),
        "dt_weight": bell_draw(splits[11], (D, SSM_HEADS), (4 * D) ** -0.5, 0.09375, ((1, 2),)),
        "conv_x": bell_draw(splits[12], (CONV_WIDTH, SSM_HEADS * SSM_HEAD_DIM), CONV_WIDTH ** -0.5, 3.0, ((1, 2),)),
        "conv_x_bias": bell_draw(splits[13], (SSM_HEADS * SSM_HEAD_DIM,), 0.5, 3.0, ((0, 2),)),
        "conv_bc": bell_draw(splits[14], (CONV_WIDTH, 2 * STATE), CONV_WIDTH ** -0.5, 3.0),
        "conv_bc_bias": bell_draw(splits[15], (2 * STATE,), 0.5, 3.0),
        "dt_bias": jnp.clip(-6.0 + 4.0 * jax.random.uniform(splits[16], (SSM_HEADS,), jnp.float32) ** shard_levels(splits[16], (SSM_HEADS,), ((0, 2),), -0.2, 0.2), -6.0, -2.0),
        "a_log": jnp.clip(2.7 * jax.random.uniform(splits[17], (SSM_HEADS,), jnp.float32) ** shard_levels(splits[17], (SSM_HEADS,), ((0, 2),), -0.2, 0.2), 0.0, 2.7),
        "skip_gain": jnp.clip(0.5 + 1.5 * jax.random.uniform(splits[18], (SSM_HEADS,), jnp.float32) ** shard_levels(splits[18], (SSM_HEADS,), ((0, 2),), -0.2, 0.2), 0.5, 2.0),
        "mixer_gain": jnp.clip(1.0 + 0.1 * jax.random.normal(splits[19], (SSM_HEADS * SSM_HEAD_DIM,), jnp.float32), 0.5, 1.5),
        "mamba_out_weight": bell_draw(splits[20], (SSM_HEADS * SSM_HEAD_DIM, D), (SSM_HEADS * SSM_HEAD_DIM) ** -0.5, 0.15625, ((0, 2),)),
        "ffn_gain": jnp.clip(1.0 + 0.1 * jax.random.normal(splits[21], (D,), jnp.float32), 0.5, 1.5),
        "gate_weight": bell_draw(splits[22], (D, FF), D ** -0.5, 0.1875, ((1, 2),)),
        "up_weight": bell_draw(splits[23], (D, FF), D ** -0.5, 0.1875, ((1, 2),)),
        "down_weight": bell_draw(splits[24], (FF, D), FF ** -0.5, 0.125, ((0, 2),)),
    }


EPSILON = 1e-05
ROPE_BASE = 100000000000.0
MASKED = -1e+30
PRECISE = lax.Precision.HIGHEST

@jax.custom_vjp
def low(v):
    return lax.optimization_barrier(v.astype(jnp.bfloat16)).astype(jnp.float32)

@jax.custom_vjp
def low_back(v):
    return v

def low_keep(v):
    return (low(v), None)

def low_pass(kept, grad):
    return (grad,)

def back_keep(v):
    return (v, None)

def back_low(kept, grad):
    return (low(grad),)
low.defvjp(low_keep, low_pass)
low_back.defvjp(back_keep, back_low)

def product(left, right):
    return jnp.dot(left, right, precision=PRECISE)

def layout(lengths_row):
    row_count = BLOCKS * BLOCK
    block_use = ((lengths_row + BLOCK - 1) // BLOCK).astype(jnp.int32)
    starts = ((jnp.cumsum(block_use) - block_use) * BLOCK).astype(jnp.int32)
    finish = starts + block_use * BLOCK
    slot_ids = jnp.arange(row_count, dtype=jnp.int32)
    inside = ((slot_ids[:, None] >= starts[None, :]) & (slot_ids[:, None] < finish[None, :])).astype(jnp.int32)
    seq_start = lax.optimization_barrier(jnp.sum(inside * starts[None, :], axis=1)).astype(jnp.int32)
    seq_length = lax.optimization_barrier(jnp.sum(inside * lengths_row[None, :], axis=1)).astype(jnp.int32)
    labels = jnp.arange(1, BLOCKS + 1, dtype=jnp.int32)
    owners = lax.optimization_barrier(jnp.sum(inside * labels[None, :], axis=1)).astype(jnp.int32)
    position = slot_ids - seq_start
    validity = (position < seq_length).astype(jnp.float32)
    carry_on = (position[::BLOCK] != 0).astype(jnp.float32)
    return (position, owners, validity, carry_on)

def rms_norm(values, gain_vector):
    scaling = lax.rsqrt(lax.optimization_barrier(jnp.mean(values * values, axis=-1, keepdims=True)) + EPSILON)
    return values * scaling * gain_vector

def rotate(values, position):
    halfway = HEAD_DIM // 2
    frequency = ROPE_BASE ** (-2.0 * jnp.arange(halfway, dtype=jnp.float32) / HEAD_DIM)
    angles = position.astype(jnp.float32)[:, None] * frequency[None, :]
    target_shape = (values.shape[0],) + (1,) * (values.ndim - 2) + (halfway,)
    cosine = jnp.cos(angles).reshape(target_shape)
    sine_part = jnp.sin(angles).reshape(target_shape)
    leading = values[..., :halfway]
    second = values[..., halfway:]
    return jnp.concatenate([leading * cosine - second * sine_part, second * cosine + leading * sine_part], axis=-1)

def convolve(values, kernel, offset_terms, position):
    summed = offset_terms[None, :] + kernel[0][None, :] * values
    for shift_by in range(1, CONV_WIDTH):
        earlier = jnp.concatenate([jnp.zeros((shift_by, values.shape[1]), values.dtype), values[:-shift_by]], axis=0)
        reached = (position >= shift_by).astype(values.dtype)
        summed = summed + kernel[shift_by][None, :] * earlier * reached[:, None]
    return jax.nn.silu(summed)

def mamba_core(inputs, bc_values, gate_lin, step_lin, step_bias, log_rates, skip_terms, norm_weight, carry_on):
    row_count, head_count = step_lin.shape
    blocks_in = row_count // BLOCK
    step_size = jax.nn.softplus(step_lin + step_bias[None, :])
    decay_rate = -jnp.exp(log_rates)
    streams = inputs.reshape(blocks_in, BLOCK, head_count, SSM_HEAD_DIM)
    write_keys = bc_values[:, :STATE].reshape(blocks_in, BLOCK, STATE)
    read_keys = bc_values[:, STATE:].reshape(blocks_in, BLOCK, STATE)
    steps_in = step_size.reshape(blocks_in, BLOCK, head_count)
    log_decay = jnp.cumsum(steps_in * decay_rate[None, None, :], axis=1)
    causal = jnp.arange(BLOCK)[:, None] >= jnp.arange(BLOCK)[None, :]
    gap_matrix = log_decay[:, :, None, :] - log_decay[:, None, :, :]
    mixing = jnp.exp(jnp.where(causal[None, :, :, None], gap_matrix, MASKED))
    intersection = jnp.einsum('ctn,csn->cts', read_keys, write_keys, precision=PRECISE)
    scaled = streams * steps_in[..., None]
    within = jnp.einsum('ctsh,cshp->cthp', intersection[..., None] * mixing, scaled, precision=PRECISE)
    to_end = jnp.exp(log_decay[:, -1:, :] - log_decay)
    pieces = jnp.einsum('csn,cshp->chnp', write_keys, scaled * to_end[..., None], precision=PRECISE)
    decays = jnp.exp(log_decay[:, -1, :])

    def advance(carried, items):
        piece_now, decay_now, keep_now = items
        entering = carried * keep_now
        return (decay_now[:, None, None] * entering + piece_now, entering)
    start_state = jnp.zeros((head_count, STATE, SSM_HEAD_DIM), jnp.float32)
    final_state, entering = lax.scan(advance, start_state, (pieces, decays, carry_on))
    across = jnp.einsum('ctn,chnp->cthp', read_keys, entering, precision=PRECISE) * jnp.exp(log_decay)[..., None]
    result = within + across + skip_terms[None, None, :, None] * streams
    gated = result * jax.nn.silu(gate_lin.reshape(blocks_in, BLOCK, head_count, SSM_HEAD_DIM))
    gated = gated.reshape(row_count, head_count * SSM_HEAD_DIM)
    scaling = lax.rsqrt(lax.optimization_barrier(jnp.mean(gated * gated, axis=-1, keepdims=True)) + EPSILON)
    return gated * scaling * norm_weight[None, :]

def attend(queries, key_rows, value_rows, owners):
    row_count = queries.shape[0]
    block_rows = min(512, row_count)
    grouping = QUERY_HEADS // KV_HEADS
    key_wide = jnp.repeat(key_rows, grouping, axis=1)
    value_wide = jnp.repeat(value_rows, grouping, axis=1)
    slot_ids = jnp.arange(row_count, dtype=jnp.int32)

    def one_block(offset):
        query_part = lax.dynamic_slice_in_dim(queries, offset, block_rows, 0)
        scores = low_back(jnp.einsum('shd,thd->hst', query_part, key_wide, precision=PRECISE) * HEAD_DIM ** (-0.5))
        query_ids = offset + jnp.arange(block_rows, dtype=jnp.int32)
        query_owner = lax.dynamic_slice_in_dim(owners, offset, block_rows, 0)
        allowed = (query_owner[:, None] == owners[None, :]) & (slot_ids[None, :] <= query_ids[:, None])
        scores = jnp.where(allowed[None], scores, MASKED)
        probabilities = low(jax.nn.softmax(scores, axis=-1))
        return jnp.einsum('hst,thd->shd', probabilities, value_wide, precision=PRECISE)
    offsets = jnp.arange(0, row_count, block_rows, dtype=jnp.int32)
    return lax.map(jax.checkpoint(one_block), offsets).reshape(row_count, QUERY_HEADS * HEAD_DIM)

def forward(tokens_wide, weight_set, position, owners, validity, carry_on):
    norm_gain, query_weight, key_weight, value_weight, attn_out_weight, z_weight, x_weight, bc_weight, dt_weight, conv_x, conv_x_bias, conv_bc, conv_bc_bias, dt_bias, a_log, skip_gain, mixer_gain, mamba_out_weight, ffn_gain, gate_weight, up_weight, down_weight = weight_set
    row_count = tokens_wide.shape[0]
    first_in = low(rms_norm(tokens_wide, norm_gain))
    query_lin = low_back(product(first_in, query_weight)).reshape(row_count, QUERY_HEADS, HEAD_DIM)
    key_lin = low_back(product(first_in, key_weight)).reshape(row_count, KV_HEADS, HEAD_DIM)
    value_lin = low_back(product(first_in, value_weight)).reshape(row_count, KV_HEADS, HEAD_DIM)
    queries = low(rotate(query_lin, position))
    key_rows = low(rotate(key_lin, position))
    value_rows = low(value_lin)
    attended = low_back(low(attend(queries, key_rows, value_rows, owners)))
    gate_lin = low_back(product(first_in, z_weight))
    stream_lin = low_back(product(first_in, x_weight))
    bc_lin = product(first_in, bc_weight)
    step_lin = low_back(product(first_in, dt_weight))
    streams = low(convolve(stream_lin, conv_x, conv_x_bias, position))
    bc_values = low(convolve(bc_lin, conv_bc, conv_bc_bias, position))
    mixed = low(mamba_core(streams, bc_values, gate_lin, step_lin, dt_bias, a_log, skip_gain, mixer_gain, carry_on))
    branch = low_back(product(attended, attn_out_weight) + product(mixed, mamba_out_weight))
    middle = tokens_wide + validity[:, None] * branch
    second_in = low(rms_norm(middle, ffn_gain))
    gate_values = low_back(product(second_in, gate_weight))
    up_values = low_back(product(second_in, up_weight))
    hidden = low(jax.nn.silu(gate_values) * up_values)
    return middle + validity[:, None] * product(hidden, down_weight)

def reference(tokens, cotangent, lengths, norm_gain, query_weight, key_weight, value_weight, attn_out_weight, z_weight, x_weight, bc_weight, dt_weight, conv_x, conv_x_bias, conv_bc, conv_bc_bias, dt_bias, a_log, skip_gain, mixer_gain, mamba_out_weight, ffn_gain, gate_weight, up_weight, down_weight):
    weight_set = tuple((weight_array.astype(jnp.float32) for weight_array in (norm_gain, query_weight, key_weight, value_weight, attn_out_weight, z_weight, x_weight, bc_weight, dt_weight, conv_x, conv_x_bias, conv_bc, conv_bc_bias, dt_bias, a_log, skip_gain, mixer_gain, mamba_out_weight, ffn_gain, gate_weight, up_weight, down_weight)))
    token_rows = tokens.astype(jnp.float32).reshape(N_DP, ROWS, D)
    cot_rows = cotangent.astype(jnp.float32).reshape(N_DP, ROWS, D)

    def per_device(totals, items):
        token_part, cot_part, length_row = items
        position, owners, validity, carry_on = layout(length_row)

        def run_layer(tokens_wide, weights_now):
            return forward(tokens_wide, weights_now, position, owners, validity, carry_on)
        result, pullback = jax.vjp(run_layer, token_part, weight_set)
        token_grad, weight_grads = pullback(cot_part)
        totals = jax.tree.map(lambda running, extra: running + extra, totals, weight_grads)
        return (totals, (result.astype(jnp.bfloat16), token_grad.astype(jnp.bfloat16)))
    start_totals = jax.tree.map(jnp.zeros_like, weight_set)
    totals, (outputs, token_grads) = lax.scan(per_device, start_totals, (token_rows, cot_rows, lengths))
    return (outputs.reshape(TOKENS, D), token_grads.reshape(TOKENS, D), totals[0], totals[1], totals[2], totals[3], totals[4], totals[5], totals[6], totals[7], totals[8], totals[9], totals[10], totals[11], totals[12], totals[13], totals[14], totals[15], totals[16], totals[17], totals[18], totals[19], totals[20], totals[21])
```

```python
from functools import partial

import jax
import jax.numpy as jnp
from jax import lax
from jax.sharding import PartitionSpec as P

SSM_HEADS = 24
SSM_HEAD_DIM = 64
STATE = 128
CONV_WIDTH = 4
HEAD_DIM = 64
BLOCK = 128


EPSILON = 1e-05
ROPE_BASE = 100000000000.0
MASKED = -1e30
PRECISE = lax.Precision.HIGHEST


def layout(lengths_row):
    row_count = lengths_row.shape[0] * BLOCK
    block_use = (lengths_row + BLOCK - 1) // BLOCK
    starts = (jnp.cumsum(block_use) - block_use) * BLOCK
    finish = starts + block_use * BLOCK
    slot_ids = jnp.arange(row_count, dtype=jnp.int32)
    inside = (
        (slot_ids[:, None] >= starts[None, :]) & (slot_ids[:, None] < finish[None, :])
    ).astype(jnp.int32)
    seq_start = jnp.sum(inside * starts[None, :], axis=1)
    seq_length = jnp.sum(inside * lengths_row[None, :], axis=1)
    labels = jnp.arange(1, lengths_row.shape[0] + 1, dtype=jnp.int32)
    owners = jnp.sum(inside * labels[None, :], axis=1)
    position = slot_ids - seq_start
    validity = (position < seq_length).astype(jnp.float32)
    carry_on = (position[::BLOCK] != 0).astype(jnp.float32)
    return (position, owners, validity, carry_on)


def project(left, right):
    return jnp.dot(left, right, preferred_element_type=jnp.float32)


def outer_rows(left, right):
    return lax.dot_general(
        left, right, (((0,), (0,)), ((), ())), preferred_element_type=jnp.float32
    )


def back_project(grad_rows, weight):
    return lax.dot_general(
        grad_rows, weight, (((1,), (1,)), ((), ())), preferred_element_type=jnp.float32
    )


def rms_norm(values, gain_vector):
    scaling = lax.rsqrt(jnp.mean(values * values, axis=-1, keepdims=True) + EPSILON)
    return values * scaling * gain_vector


def swiglu(gate_values, up_values):
    return jax.nn.silu(gate_values) * up_values


def rotate(values, position):
    halfway = HEAD_DIM // 2
    frequency = ROPE_BASE ** (-2.0 * jnp.arange(halfway, dtype=jnp.float32) / HEAD_DIM)
    angles = position.astype(jnp.float32)[:, None] * frequency[None, :]
    target_shape = (values.shape[0],) + (1,) * (values.ndim - 2) + (halfway,)
    cosine = jnp.cos(angles).reshape(target_shape)
    sine_part = jnp.sin(angles).reshape(target_shape)
    leading = values[..., :halfway]
    second = values[..., halfway:]
    return jnp.concatenate(
        [leading * cosine - second * sine_part, second * cosine + leading * sine_part], axis=-1
    )


def convolve(values, kernel, offset_terms, position):
    summed = offset_terms[None, :] + kernel[0][None, :] * values
    for shift_by in range(1, CONV_WIDTH):
        earlier = jnp.concatenate(
            [jnp.zeros((shift_by, values.shape[1]), values.dtype), values[:-shift_by]], axis=0
        )
        reached = (position >= shift_by).astype(values.dtype)
        summed = summed + kernel[shift_by][None, :] * earlier * reached[:, None]
    return jax.nn.silu(summed)


def mamba_core(inputs, bc_values, gate_lin, step_lin, step_bias, log_rates, skip_terms, carry_on):
    row_count, head_count = step_lin.shape
    blocks_in = row_count // BLOCK
    step_size = jax.nn.softplus(step_lin + step_bias[None, :])
    decay_rate = -jnp.exp(log_rates)
    streams = inputs.reshape(blocks_in, BLOCK, head_count, SSM_HEAD_DIM)
    write_keys = bc_values[:, :STATE].reshape(blocks_in, BLOCK, STATE)
    read_keys = bc_values[:, STATE:].reshape(blocks_in, BLOCK, STATE)
    steps_in = step_size.reshape(blocks_in, BLOCK, head_count)
    log_decay = jnp.cumsum(steps_in * decay_rate[None, None, :], axis=1)
    causal = jnp.arange(BLOCK)[:, None] >= jnp.arange(BLOCK)[None, :]
    gap_matrix = log_decay[:, :, None, :] - log_decay[:, None, :, :]
    mixing = jnp.exp(jnp.where(causal[None, :, :, None], gap_matrix, MASKED))
    intersection = jnp.einsum("ctn,csn->cts", read_keys, write_keys, precision=PRECISE)
    scaled = streams * steps_in[..., None]
    within = jnp.einsum(
        "ctsh,cshp->cthp", intersection[..., None] * mixing, scaled, precision=PRECISE
    )
    to_end = jnp.exp(log_decay[:, -1:, :] - log_decay)
    pieces = jnp.einsum("csn,cshp->chnp", write_keys, scaled * to_end[..., None], precision=PRECISE)
    decays = jnp.exp(log_decay[:, -1, :])

    def advance(carried, items):
        piece_now, decay_now, keep_now = items
        entering = carried * keep_now
        return (decay_now[:, None, None] * entering + piece_now, entering)

    start_state = jnp.zeros((head_count, STATE, SSM_HEAD_DIM), jnp.float32)
    final_state, entering = lax.scan(advance, start_state, (pieces, decays, carry_on))
    across = (
        jnp.einsum("ctn,chnp->cthp", read_keys, entering, precision=PRECISE)
        * jnp.exp(log_decay)[..., None]
    )
    result = within + across + skip_terms[None, None, :, None] * streams
    gated = result * jax.nn.silu(gate_lin.reshape(blocks_in, BLOCK, head_count, SSM_HEAD_DIM))
    return gated.reshape(row_count, head_count * SSM_HEAD_DIM)


def block_scores(query_part, key_rows, owners, offset, slot_ids):
    block_rows = query_part.shape[0]
    scores = jnp.einsum(
        "shgd,thd->hgst", query_part, key_rows, preferred_element_type=jnp.float32
    ) * HEAD_DIM ** (-0.5)
    query_ids = offset + jnp.arange(block_rows, dtype=jnp.int32)
    query_owner = lax.dynamic_slice_in_dim(owners, offset, block_rows, 0)
    allowed = (query_owner[:, None] == owners[None, :]) & (slot_ids[None, :] <= query_ids[:, None])
    return jnp.where(allowed, scores, MASKED)


def attend_forward(queries, key_rows, value_rows, owners):
    row_count = queries.shape[0]
    block_rows = min(512, row_count)
    slot_ids = jnp.arange(row_count, dtype=jnp.int32)

    def one_block(offset):
        query_part = lax.dynamic_slice_in_dim(queries, offset, block_rows, 0)
        scores = block_scores(query_part, key_rows, owners, offset, slot_ids)
        maxima = jnp.max(scores, axis=-1, keepdims=True)
        expo = jnp.exp(scores - maxima)
        totals = jnp.sum(expo, axis=-1, keepdims=True)
        probabilities = (expo / totals).astype(jnp.bfloat16)
        result = jnp.einsum(
            "hgst,thd->shgd", probabilities, value_rows, preferred_element_type=jnp.float32
        )
        return (result, (maxima + jnp.log(totals))[..., 0])

    offsets = jnp.arange(0, row_count, block_rows, dtype=jnp.int32)
    results, log_totals = lax.map(one_block, offsets)
    return (results.reshape(queries.shape), log_totals)


def attend_backward(queries, key_rows, value_rows, owners, log_totals, grad_out):
    row_count = queries.shape[0]
    block_rows = min(512, row_count)
    slot_ids = jnp.arange(row_count, dtype=jnp.int32)
    score_scale = HEAD_DIM ** (-0.5)

    def one_block(carried, items):
        key_grad, value_grad = carried
        offset, totals = items
        query_part = lax.dynamic_slice_in_dim(queries, offset, block_rows, 0)
        grad_part = lax.dynamic_slice_in_dim(grad_out, offset, block_rows, 0)
        scores = block_scores(query_part, key_rows, owners, offset, slot_ids)
        probabilities = jnp.exp(scores - totals[..., None])
        value_grad = value_grad + jnp.einsum(
            "hgst,shgd->thd",
            probabilities.astype(jnp.bfloat16),
            grad_part,
            preferred_element_type=jnp.float32,
        )
        prob_grad = jnp.einsum(
            "shgd,thd->hgst", grad_part, value_rows, preferred_element_type=jnp.float32
        )
        score_grad_low = (
            probabilities * (prob_grad - jnp.sum(probabilities * prob_grad, axis=-1, keepdims=True))
        ).astype(jnp.bfloat16)
        query_grad = (
            jnp.einsum(
                "hgst,thd->shgd", score_grad_low, key_rows, preferred_element_type=jnp.float32
            )
            * score_scale
        )
        key_grad = (
            key_grad
            + jnp.einsum(
                "hgst,shgd->thd", score_grad_low, query_part, preferred_element_type=jnp.float32
            )
            * score_scale
        )
        return ((key_grad, value_grad), query_grad)

    offsets = jnp.arange(0, row_count, block_rows, dtype=jnp.int32)
    zeros_kv = jnp.zeros(key_rows.shape, jnp.float32)
    (key_grad, value_grad), query_grads = lax.scan(
        one_block, (zeros_kv, zeros_kv), (offsets, log_totals)
    )
    return (query_grads.reshape(queries.shape), key_grad, value_grad)


def dp_sum(row_split, col_split, vectors):
    n_dp = lax.axis_size("dp")
    pieces = [g.reshape(n_dp, -1) for g in row_split]
    pieces += [
        g.reshape(g.shape[0], n_dp, g.shape[1] // n_dp).transpose(1, 0, 2).reshape(n_dp, -1)
        for g in col_split
    ]
    pieces += [jnp.broadcast_to(v.reshape(1, -1), (n_dp, v.size)) for v in vectors]
    widths = [p.shape[1] for p in pieces]
    lane_rows = -(-sum(widths) // 16384) * 128
    pieces.append(jnp.zeros((n_dp, lane_rows * 128 - sum(widths)), jnp.float32))
    packed = lax.psum_scatter(
        jnp.concatenate(pieces, axis=1).reshape(n_dp * lane_rows, 128),
        "dp",
        scatter_dimension=0,
        tiled=True,
    ).reshape(-1)
    shapes = [(g.shape[0] // n_dp, g.shape[1]) for g in row_split]
    shapes += [(g.shape[0], g.shape[1] // n_dp) for g in col_split]
    shapes += [v.shape for v in vectors]
    outs = []
    at = 0
    for w, s in zip(widths, shapes):
        outs.append(packed[at : at + w].reshape(s))
        at += w
    return outs


def body(
    tokens,
    cotangent,
    lengths,
    norm_gain,
    query_weight,
    key_weight,
    value_weight,
    attn_out_weight,
    z_weight,
    x_weight,
    bc_weight,
    dt_weight,
    conv_x,
    conv_x_bias,
    conv_bc,
    conv_bc_bias,
    dt_bias,
    a_log,
    skip_gain,
    mixer_gain,
    mamba_out_weight,
    ffn_gain,
    gate_weight,
    up_weight,
    down_weight,
):
    position, owners, validity, carry_on = layout(lengths[0])
    row_count = tokens.shape[0]
    kv_local = key_weight.shape[1] // HEAD_DIM
    grouping = query_weight.shape[1] // key_weight.shape[1]
    group_width = SSM_HEADS * SSM_HEAD_DIM
    valid_col = validity[:, None]
    tokens_wide = tokens.astype(jnp.float32)
    normed, first_norm_back = jax.vjp(rms_norm, tokens_wide, norm_gain)
    first_in = normed.astype(jnp.bfloat16)
    rotation = partial(rotate, position=position)
    query_lin = project(first_in, query_weight).reshape(row_count, kv_local, grouping, HEAD_DIM)
    key_lin = project(first_in, key_weight).reshape(row_count, kv_local, HEAD_DIM)
    value_rows = (
        project(first_in, value_weight).reshape(row_count, kv_local, HEAD_DIM).astype(jnp.bfloat16)
    )
    query_turned, query_unturn = jax.vjp(rotation, query_lin)
    key_turned, key_unturn = jax.vjp(rotation, key_lin)
    queries = query_turned.astype(jnp.bfloat16)
    key_rows = key_turned.astype(jnp.bfloat16)
    attended_wide, log_totals = attend_forward(queries, key_rows, value_rows, owners)
    attended = attended_wide.reshape(row_count, -1).astype(jnp.bfloat16)
    gate_lin = project(first_in, z_weight)
    stream_lin = project(first_in, x_weight)
    bc_lin = project(first_in, bc_weight)
    step_lin = project(first_in, dt_weight)
    causal_filter = partial(convolve, position=position)
    streams_wide, stream_back = jax.vjp(
        causal_filter, stream_lin, conv_x.astype(jnp.float32), conv_x_bias.astype(jnp.float32)
    )
    bc_wide, bc_back = jax.vjp(
        causal_filter, bc_lin, conv_bc.astype(jnp.float32), conv_bc_bias.astype(jnp.float32)
    )
    streams = streams_wide.astype(jnp.bfloat16)
    bc_values = bc_wide.astype(jnp.bfloat16)
    ssm_core = partial(mamba_core, carry_on=carry_on)
    gated_wide, core_back = jax.vjp(
        ssm_core,
        streams.astype(jnp.float32),
        bc_values.astype(jnp.float32),
        gate_lin,
        step_lin,
        dt_bias,
        a_log,
        skip_gain,
    )
    square_sum = lax.psum(jnp.sum(gated_wide * gated_wide, axis=-1), "tensor")
    group_scale = lax.rsqrt(square_sum / group_width + EPSILON)[:, None]
    normed_gated = gated_wide * group_scale
    mixed = (normed_gated * mixer_gain[None, :]).astype(jnp.bfloat16)
    branch_part = project(attended, attn_out_weight) + project(mixed, mamba_out_weight)
    branch = lax.psum(branch_part, "tensor")
    middle = tokens_wide + valid_col * branch
    second_wide, second_norm_back = jax.vjp(rms_norm, middle, ffn_gain)
    second_in = second_wide.astype(jnp.bfloat16)
    gate_values = project(second_in, gate_weight)
    up_values = project(second_in, up_weight)
    hidden_wide, hidden_back = jax.vjp(swiglu, gate_values, up_values)
    hidden = hidden_wide.astype(jnp.bfloat16)
    ffn_full = lax.psum(project(hidden, down_weight), "tensor")
    block_output = (middle + valid_col * ffn_full).astype(jnp.bfloat16)
    cot_wide = cotangent.astype(jnp.float32)
    grad_ffn = (valid_col * cot_wide).astype(jnp.bfloat16)
    down_grad = outer_rows(hidden, grad_ffn)
    grad_hidden = back_project(grad_ffn, down_weight)
    grad_gate_wide, grad_up_wide = hidden_back(grad_hidden)
    grad_gate = grad_gate_wide.astype(jnp.bfloat16)
    grad_up = grad_up_wide.astype(jnp.bfloat16)
    gate_grad = outer_rows(second_in, grad_gate)
    up_grad = outer_rows(second_in, grad_up)
    grad_second = lax.psum(
        back_project(grad_gate, gate_weight) + back_project(grad_up, up_weight), "tensor"
    )
    grad_middle_norm, ffn_gain_grad = second_norm_back(grad_second)
    grad_middle = cot_wide + grad_middle_norm
    grad_branch = (valid_col * grad_middle).astype(jnp.bfloat16)
    attn_out_grad = outer_rows(attended, grad_branch)
    mamba_out_grad = outer_rows(mixed, grad_branch)
    grad_attended = (
        back_project(grad_branch, attn_out_weight)
        .astype(jnp.bfloat16)
        .reshape(row_count, kv_local, grouping, HEAD_DIM)
    )
    grad_mixed = back_project(grad_branch, mamba_out_weight)
    gain_scaled = grad_mixed * mixer_gain[None, :]
    mixer_gain_grad = jnp.sum(grad_mixed * normed_gated, axis=0)
    cross_sum = lax.psum(jnp.sum(gain_scaled * normed_gated, axis=-1), "tensor")
    grad_gated = group_scale * (gain_scaled - normed_gated * (cross_sum / group_width)[:, None])
    grad_streams, grad_bc, grad_gate_lin, grad_step_lin, dt_bias_grad, a_log_grad, skip_grad = (
        core_back(grad_gated)
    )
    grad_stream_lin, conv_x_grad, conv_x_bias_grad = stream_back(grad_streams)
    grad_bc_lin, conv_bc_part, conv_bc_bias_part = bc_back(grad_bc)
    grad_query, grad_key, grad_value = attend_backward(
        queries, key_rows, value_rows, owners, log_totals, grad_attended
    )
    (grad_query_lin,) = query_unturn(grad_query)
    (grad_key_lin,) = key_unturn(grad_key)
    grad_query_low = grad_query_lin.reshape(row_count, -1).astype(jnp.bfloat16)
    grad_key_low = grad_key_lin.reshape(row_count, -1).astype(jnp.bfloat16)
    grad_value_low = grad_value.reshape(row_count, -1).astype(jnp.bfloat16)
    grad_gate_low = grad_gate_lin.astype(jnp.bfloat16)
    grad_stream_low = grad_stream_lin.astype(jnp.bfloat16)
    grad_step_low = grad_step_lin.astype(jnp.bfloat16)
    query_grad = outer_rows(first_in, grad_query_low)
    key_grad = outer_rows(first_in, grad_key_low)
    value_grad = outer_rows(first_in, grad_value_low)
    z_grad = outer_rows(first_in, grad_gate_low)
    x_grad = outer_rows(first_in, grad_stream_low)
    dt_grad = outer_rows(first_in, grad_step_low)
    bc_part = lax.dot_general(
        first_in.astype(jnp.float32), grad_bc_lin, (((0,), (0,)), ((), ())), precision=PRECISE
    )
    grad_first_part = (
        back_project(grad_query_low, query_weight)
        + back_project(grad_key_low, key_weight)
        + back_project(grad_value_low, value_weight)
        + back_project(grad_gate_low, z_weight)
        + back_project(grad_stream_low, x_weight)
        + back_project(grad_step_low, dt_weight)
        + lax.dot_general(
            grad_bc_lin, bc_weight.astype(jnp.float32), (((1,), (1,)), ((), ())), precision=PRECISE
        )
    )
    grad_first, bc_grad_full, conv_bc_grad, conv_bc_bias_grad = lax.psum(
        (grad_first_part, bc_part, conv_bc_part, conv_bc_bias_part), "tensor"
    )
    grad_tokens_norm, norm_gain_grad = first_norm_back(grad_first)
    tokens_grad = (grad_middle + grad_tokens_norm).astype(jnp.bfloat16)
    early = dp_sum((gate_grad, up_grad), (attn_out_grad, mamba_out_grad, down_grad), ())
    late = dp_sum(
        (query_grad, key_grad, value_grad, z_grad, x_grad, bc_grad_full, dt_grad),
        (),
        (
            norm_gain_grad,
            conv_x_grad,
            conv_x_bias_grad,
            conv_bc_grad,
            conv_bc_bias_grad,
            dt_bias_grad,
            a_log_grad,
            skip_grad,
            mixer_gain_grad,
            ffn_gain_grad,
        ),
    )
    matrix_sums = (
        late[0],
        late[1],
        late[2],
        early[2],
        late[3],
        late[4],
        late[5],
        late[6],
        early[3],
        early[0],
        early[1],
        early[4],
    )
    vector_sums = late[7:]
    return (
        block_output,
        tokens_grad,
        vector_sums[0],
        matrix_sums[0],
        matrix_sums[1],
        matrix_sums[2],
        matrix_sums[3],
        matrix_sums[4],
        matrix_sums[5],
        matrix_sums[6],
        matrix_sums[7],
        vector_sums[1],
        vector_sums[2],
        vector_sums[3],
        vector_sums[4],
        vector_sums[5],
        vector_sums[6],
        vector_sums[7],
        vector_sums[8],
        matrix_sums[8],
        vector_sums[9],
        matrix_sums[9],
        matrix_sums[10],
        matrix_sums[11],
    )


def solution(mesh):
    return jax.shard_map(
        body,
        mesh=mesh,
        in_specs=(
            P("dp", None),
            P("dp", None),
            P("dp", None),
            P(),
            P(None, "tensor"),
            P(None, "tensor"),
            P(None, "tensor"),
            P("tensor", None),
            P(None, "tensor"),
            P(None, "tensor"),
            P(),
            P(None, "tensor"),
            P(None, "tensor"),
            P("tensor"),
            P(),
            P(),
            P("tensor"),
            P("tensor"),
            P("tensor"),
            P("tensor"),
            P("tensor", None),
            P(),
            P(None, "tensor"),
            P(None, "tensor"),
            P("tensor", None),
        ),
        out_specs=(
            P("dp", None),
            P("dp", None),
            P(),
            P("dp", "tensor"),
            P("dp", "tensor"),
            P("dp", "tensor"),
            P("tensor", "dp"),
            P("dp", "tensor"),
            P("dp", "tensor"),
            P("dp", None),
            P("dp", "tensor"),
            P(None, "tensor"),
            P("tensor"),
            P(),
            P(),
            P("tensor"),
            P("tensor"),
            P("tensor"),
            P("tensor"),
            P("tensor", "dp"),
            P(),
            P("dp", "tensor"),
            P("dp", "tensor"),
            P("tensor", "dp"),
        ),
        check_vma=False,
    )
```

```python
from functools import partial

import jax
import jax.numpy as jnp
from jax import lax
from jax.sharding import PartitionSpec as P

SSM_HEADS = 24
SSM_HEAD_DIM = 64
STATE = 128
CONV_WIDTH = 4
HEAD_DIM = 64
BLOCK = 128


EPSILON = 1e-05
ROPE_BASE = 100000000000.0
MASKED = -1e30
PRECISE = lax.Precision.HIGHEST


def layout(lengths_row):
    row_count = lengths_row.shape[0] * BLOCK
    block_use = (lengths_row + BLOCK - 1) // BLOCK
    starts = (jnp.cumsum(block_use) - block_use) * BLOCK
    finish = starts + block_use * BLOCK
    slot_ids = jnp.arange(row_count, dtype=jnp.int32)
    inside = (
        (slot_ids[:, None] >= starts[None, :]) & (slot_ids[:, None] < finish[None, :])
    ).astype(jnp.int32)
    seq_start = jnp.sum(inside * starts[None, :], axis=1)
    seq_length = jnp.sum(inside * lengths_row[None, :], axis=1)
    labels = jnp.arange(1, lengths_row.shape[0] + 1, dtype=jnp.int32)
    owners = jnp.sum(inside * labels[None, :], axis=1)
    position = slot_ids - seq_start
    validity = (position < seq_length).astype(jnp.float32)
    carry_on = (position[::BLOCK] != 0).astype(jnp.float32)
    return (position, owners, validity, carry_on)


def project(left, right):
    return jnp.dot(left, right, preferred_element_type=jnp.float32)


def outer_rows(left, right):
    return lax.dot_general(
        left, right, (((0,), (0,)), ((), ())), preferred_element_type=jnp.float32
    )


def back_project(grad_rows, weight):
    return lax.dot_general(
        grad_rows, weight, (((1,), (1,)), ((), ())), preferred_element_type=jnp.float32
    )


def rms_norm(values, gain_vector):
    scaling = lax.rsqrt(jnp.mean(values * values, axis=-1, keepdims=True) + EPSILON)
    return values * scaling * gain_vector


def swiglu(gate_values, up_values):
    return jax.nn.silu(gate_values) * up_values


def rotate(values, position):
    halfway = HEAD_DIM // 2
    frequency = ROPE_BASE ** (-2.0 * jnp.arange(halfway, dtype=jnp.float32) / HEAD_DIM)
    angles = position.astype(jnp.float32)[:, None] * frequency[None, :]
    target_shape = (values.shape[0],) + (1,) * (values.ndim - 2) + (halfway,)
    cosine = jnp.cos(angles).reshape(target_shape)
    sine_part = jnp.sin(angles).reshape(target_shape)
    leading = values[..., :halfway]
    second = values[..., halfway:]
    return jnp.concatenate(
        [leading * cosine - second * sine_part, second * cosine + leading * sine_part], axis=-1
    )


def convolve(values, kernel, offset_terms, position):
    summed = offset_terms[None, :] + kernel[0][None, :] * values
    for shift_by in range(1, CONV_WIDTH):
        earlier = jnp.concatenate(
            [jnp.zeros((shift_by, values.shape[1]), values.dtype), values[:-shift_by]], axis=0
        )
        reached = (position >= shift_by).astype(values.dtype)
        summed = summed + kernel[shift_by][None, :] * earlier * reached[:, None]
    return jax.nn.silu(summed)


def mamba_core(inputs, bc_values, gate_lin, step_lin, step_bias, log_rates, skip_terms, carry_on):
    row_count, head_count = step_lin.shape
    blocks_in = row_count // BLOCK
    step_size = jax.nn.softplus(step_lin + step_bias[None, :])
    decay_rate = -jnp.exp(log_rates)
    streams = inputs.reshape(blocks_in, BLOCK, head_count, SSM_HEAD_DIM)
    write_keys = bc_values[:, :STATE].reshape(blocks_in, BLOCK, STATE)
    read_keys = bc_values[:, STATE:].reshape(blocks_in, BLOCK, STATE)
    steps_in = step_size.reshape(blocks_in, BLOCK, head_count)
    log_decay = jnp.cumsum(steps_in * decay_rate[None, None, :], axis=1)
    causal = jnp.arange(BLOCK)[:, None] >= jnp.arange(BLOCK)[None, :]
    gap_matrix = log_decay[:, :, None, :] - log_decay[:, None, :, :]
    mixing = jnp.exp(jnp.where(causal[None, :, :, None], gap_matrix, MASKED))
    intersection = jnp.einsum("ctn,csn->cts", read_keys, write_keys, precision=PRECISE)
    scaled = streams * steps_in[..., None]
    within = jnp.einsum(
        "ctsh,cshp->cthp", intersection[..., None] * mixing, scaled, precision=PRECISE
    )
    to_end = jnp.exp(log_decay[:, -1:, :] - log_decay)
    pieces = jnp.einsum("csn,cshp->chnp", write_keys, scaled * to_end[..., None], precision=PRECISE)
    decays = jnp.exp(log_decay[:, -1, :])

    def advance(carried, items):
        piece_now, decay_now, keep_now = items
        entering = carried * keep_now
        return (decay_now[:, None, None] * entering + piece_now, entering)

    start_state = jnp.zeros((head_count, STATE, SSM_HEAD_DIM), jnp.float32)
    final_state, entering = lax.scan(advance, start_state, (pieces, decays, carry_on))
    across = (
        jnp.einsum("ctn,chnp->cthp", read_keys, entering, precision=PRECISE)
        * jnp.exp(log_decay)[..., None]
    )
    result = within + across + skip_terms[None, None, :, None] * streams
    gated = result * jax.nn.silu(gate_lin.reshape(blocks_in, BLOCK, head_count, SSM_HEAD_DIM))
    return gated.reshape(row_count, head_count * SSM_HEAD_DIM)


def block_scores(query_part, key_rows, owners, offset, slot_ids):
    block_rows = query_part.shape[0]
    scores = jnp.einsum(
        "shgd,thd->hgst", query_part, key_rows, preferred_element_type=jnp.float32
    ) * HEAD_DIM ** (-0.5)
    query_ids = offset + jnp.arange(block_rows, dtype=jnp.int32)
    query_owner = lax.dynamic_slice_in_dim(owners, offset, block_rows, 0)
    allowed = (query_owner[:, None] == owners[None, :]) & (slot_ids[None, :] <= query_ids[:, None])
    return jnp.where(allowed, scores, MASKED)


def attend_forward(queries, key_rows, value_rows, owners):
    row_count = queries.shape[0]
    block_rows = min(512, row_count)
    slot_ids = jnp.arange(row_count, dtype=jnp.int32)

    def one_block(offset):
        query_part = lax.dynamic_slice_in_dim(queries, offset, block_rows, 0)
        scores = block_scores(query_part, key_rows, owners, offset, slot_ids)
        maxima = jnp.max(scores, axis=-1, keepdims=True)
        expo = jnp.exp(scores - maxima)
        totals = jnp.sum(expo, axis=-1, keepdims=True)
        probabilities = (expo / totals).astype(jnp.bfloat16)
        result = jnp.einsum(
            "hgst,thd->shgd", probabilities, value_rows, preferred_element_type=jnp.float32
        )
        return (result, (maxima + jnp.log(totals))[..., 0])

    offsets = jnp.arange(0, row_count, block_rows, dtype=jnp.int32)
    results, log_totals = lax.map(one_block, offsets)
    return (results.reshape(queries.shape), log_totals)


def attend_backward(queries, key_rows, value_rows, owners, log_totals, grad_out):
    row_count = queries.shape[0]
    block_rows = min(512, row_count)
    slot_ids = jnp.arange(row_count, dtype=jnp.int32)
    score_scale = HEAD_DIM ** (-0.5)

    def one_block(carried, items):
        key_grad, value_grad = carried
        offset, totals = items
        query_part = lax.dynamic_slice_in_dim(queries, offset, block_rows, 0)
        grad_part = lax.dynamic_slice_in_dim(grad_out, offset, block_rows, 0)
        scores = block_scores(query_part, key_rows, owners, offset, slot_ids)
        probabilities = jnp.exp(scores - totals[..., None])
        value_grad = value_grad + jnp.einsum(
            "hgst,shgd->thd",
            probabilities.astype(jnp.bfloat16),
            grad_part,
            preferred_element_type=jnp.float32,
        )
        prob_grad = jnp.einsum(
            "shgd,thd->hgst", grad_part, value_rows, preferred_element_type=jnp.float32
        )
        score_grad_low = (
            probabilities * (prob_grad - jnp.sum(probabilities * prob_grad, axis=-1, keepdims=True))
        ).astype(jnp.bfloat16)
        query_grad = (
            jnp.einsum(
                "hgst,thd->shgd", score_grad_low, key_rows, preferred_element_type=jnp.float32
            )
            * score_scale
        )
        key_grad = (
            key_grad
            + jnp.einsum(
                "hgst,shgd->thd", score_grad_low, query_part, preferred_element_type=jnp.float32
            )
            * score_scale
        )
        return ((key_grad, value_grad), query_grad)

    offsets = jnp.arange(0, row_count, block_rows, dtype=jnp.int32)
    zeros_kv = jnp.zeros(key_rows.shape, jnp.float32)
    (key_grad, value_grad), query_grads = lax.scan(
        one_block, (zeros_kv, zeros_kv), (offsets, log_totals)
    )
    return (query_grads.reshape(queries.shape), key_grad, value_grad)


def tensor_sum(values):
    if lax.axis_size("tensor") != 2:
        return lax.psum(values, "tensor")
    swapped = lax.ppermute(values, "tensor", perm=[(0, 1), (1, 0)])
    return jax.tree.map(lambda mine, theirs: mine + theirs, values, swapped)


def dp_sum(row_split, col_split, vectors):
    n_dp = lax.axis_size("dp")
    pieces = [g.reshape(n_dp, -1) for g in row_split]
    pieces += [
        g.reshape(g.shape[0], n_dp, g.shape[1] // n_dp).transpose(1, 0, 2).reshape(n_dp, -1)
        for g in col_split
    ]
    pieces += [jnp.broadcast_to(v.reshape(1, -1), (n_dp, v.size)) for v in vectors]
    widths = [p.shape[1] for p in pieces]
    lane_rows = -(-sum(widths) // 16384) * 128
    pieces.append(jnp.zeros((n_dp, lane_rows * 128 - sum(widths)), jnp.float32))
    packed = lax.psum_scatter(
        jnp.concatenate(pieces, axis=1).reshape(n_dp * lane_rows, 128),
        "dp",
        scatter_dimension=0,
        tiled=True,
    ).reshape(-1)
    shapes = [(g.shape[0] // n_dp, g.shape[1]) for g in row_split]
    shapes += [(g.shape[0], g.shape[1] // n_dp) for g in col_split]
    shapes += [v.shape for v in vectors]
    outs = []
    at = 0
    for w, s in zip(widths, shapes):
        outs.append(packed[at : at + w].reshape(s))
        at += w
    return outs


def body(
    tokens,
    cotangent,
    lengths,
    norm_gain,
    query_weight,
    key_weight,
    value_weight,
    attn_out_weight,
    z_weight,
    x_weight,
    bc_weight,
    dt_weight,
    conv_x,
    conv_x_bias,
    conv_bc,
    conv_bc_bias,
    dt_bias,
    a_log,
    skip_gain,
    mixer_gain,
    mamba_out_weight,
    ffn_gain,
    gate_weight,
    up_weight,
    down_weight,
):
    position, owners, validity, carry_on = layout(lengths[0])
    row_count = tokens.shape[0]
    kv_local = key_weight.shape[1] // HEAD_DIM
    grouping = query_weight.shape[1] // key_weight.shape[1]
    group_width = SSM_HEADS * SSM_HEAD_DIM
    valid_col = validity[:, None]
    tokens_wide = tokens.astype(jnp.float32)
    normed, first_norm_back = jax.vjp(rms_norm, tokens_wide, norm_gain)
    first_in = normed.astype(jnp.bfloat16)
    rotation = partial(rotate, position=position)
    query_lin = project(first_in, query_weight).reshape(row_count, kv_local, grouping, HEAD_DIM)
    key_lin = project(first_in, key_weight).reshape(row_count, kv_local, HEAD_DIM)
    value_rows = (
        project(first_in, value_weight).reshape(row_count, kv_local, HEAD_DIM).astype(jnp.bfloat16)
    )
    query_turned, query_unturn = jax.vjp(rotation, query_lin)
    key_turned, key_unturn = jax.vjp(rotation, key_lin)
    queries = query_turned.astype(jnp.bfloat16)
    key_rows = key_turned.astype(jnp.bfloat16)
    attended_wide, log_totals = attend_forward(queries, key_rows, value_rows, owners)
    attended = attended_wide.reshape(row_count, -1).astype(jnp.bfloat16)
    gate_lin = project(first_in, z_weight)
    stream_lin = project(first_in, x_weight)
    bc_lin = project(first_in, bc_weight)
    step_lin = project(first_in, dt_weight)
    causal_filter = partial(convolve, position=position)
    streams_wide, stream_back = jax.vjp(
        causal_filter, stream_lin, conv_x.astype(jnp.float32), conv_x_bias.astype(jnp.float32)
    )
    bc_wide, bc_back = jax.vjp(
        causal_filter, bc_lin, conv_bc.astype(jnp.float32), conv_bc_bias.astype(jnp.float32)
    )
    streams = streams_wide.astype(jnp.bfloat16)
    bc_values = bc_wide.astype(jnp.bfloat16)
    ssm_core = partial(mamba_core, carry_on=carry_on)
    gated_wide, core_back = jax.vjp(
        ssm_core,
        streams.astype(jnp.float32),
        bc_values.astype(jnp.float32),
        gate_lin,
        step_lin,
        dt_bias,
        a_log,
        skip_gain,
    )
    square_sum = lax.psum(jnp.sum(gated_wide * gated_wide, axis=-1), "tensor")
    group_scale = lax.rsqrt(square_sum / group_width + EPSILON)[:, None]
    normed_gated = gated_wide * group_scale
    mixed = (normed_gated * mixer_gain[None, :]).astype(jnp.bfloat16)
    branch_part = project(attended, attn_out_weight) + project(mixed, mamba_out_weight)
    branch = tensor_sum(branch_part)
    middle = tokens_wide + valid_col * branch
    second_wide, second_norm_back = jax.vjp(rms_norm, middle, ffn_gain)
    second_in = second_wide.astype(jnp.bfloat16)
    gate_values = project(second_in, gate_weight)
    up_values = project(second_in, up_weight)
    hidden_wide, hidden_back = jax.vjp(swiglu, gate_values, up_values)
    hidden = hidden_wide.astype(jnp.bfloat16)
    ffn_full = tensor_sum(project(hidden, down_weight))
    block_output = (middle + valid_col * ffn_full).astype(jnp.bfloat16)
    cot_wide = cotangent.astype(jnp.float32)
    grad_ffn = (valid_col * cot_wide).astype(jnp.bfloat16)
    down_grad = outer_rows(hidden, grad_ffn)
    grad_hidden = back_project(grad_ffn, down_weight)
    grad_gate_wide, grad_up_wide = hidden_back(grad_hidden)
    grad_gate = grad_gate_wide.astype(jnp.bfloat16)
    grad_up = grad_up_wide.astype(jnp.bfloat16)
    gate_grad = outer_rows(second_in, grad_gate)
    up_grad = outer_rows(second_in, grad_up)
    grad_second = tensor_sum(
        back_project(grad_gate, gate_weight) + back_project(grad_up, up_weight)
    )
    grad_middle_norm, ffn_gain_grad = second_norm_back(grad_second)
    grad_middle = cot_wide + grad_middle_norm
    grad_branch = (valid_col * grad_middle).astype(jnp.bfloat16)
    attn_out_grad = outer_rows(attended, grad_branch)
    mamba_out_grad = outer_rows(mixed, grad_branch)
    grad_attended = (
        back_project(grad_branch, attn_out_weight)
        .astype(jnp.bfloat16)
        .reshape(row_count, kv_local, grouping, HEAD_DIM)
    )
    grad_mixed = back_project(grad_branch, mamba_out_weight)
    gain_scaled = grad_mixed * mixer_gain[None, :]
    mixer_gain_grad = jnp.sum(grad_mixed * normed_gated, axis=0)
    cross_sum = lax.psum(jnp.sum(gain_scaled * normed_gated, axis=-1), "tensor")
    grad_gated = group_scale * (gain_scaled - normed_gated * (cross_sum / group_width)[:, None])
    grad_streams, grad_bc, grad_gate_lin, grad_step_lin, dt_bias_grad, a_log_grad, skip_grad = (
        core_back(grad_gated)
    )
    grad_stream_lin, conv_x_grad, conv_x_bias_grad = stream_back(grad_streams)
    grad_bc_lin, conv_bc_part, conv_bc_bias_part = bc_back(grad_bc)
    grad_query, grad_key, grad_value = attend_backward(
        queries, key_rows, value_rows, owners, log_totals, grad_attended
    )
    (grad_query_lin,) = query_unturn(grad_query)
    (grad_key_lin,) = key_unturn(grad_key)
    grad_query_low = grad_query_lin.reshape(row_count, -1).astype(jnp.bfloat16)
    grad_key_low = grad_key_lin.reshape(row_count, -1).astype(jnp.bfloat16)
    grad_value_low = grad_value.reshape(row_count, -1).astype(jnp.bfloat16)
    grad_gate_low = grad_gate_lin.astype(jnp.bfloat16)
    grad_stream_low = grad_stream_lin.astype(jnp.bfloat16)
    grad_step_low = grad_step_lin.astype(jnp.bfloat16)
    query_grad = outer_rows(first_in, grad_query_low)
    key_grad = outer_rows(first_in, grad_key_low)
    value_grad = outer_rows(first_in, grad_value_low)
    z_grad = outer_rows(first_in, grad_gate_low)
    x_grad = outer_rows(first_in, grad_stream_low)
    dt_grad = outer_rows(first_in, grad_step_low)
    bc_part = lax.dot_general(
        first_in.astype(jnp.float32), grad_bc_lin, (((0,), (0,)), ((), ())), precision=PRECISE
    )
    grad_first_part = (
        back_project(grad_query_low, query_weight)
        + back_project(grad_key_low, key_weight)
        + back_project(grad_value_low, value_weight)
        + back_project(grad_gate_low, z_weight)
        + back_project(grad_stream_low, x_weight)
        + back_project(grad_step_low, dt_weight)
        + lax.dot_general(
            grad_bc_lin, bc_weight.astype(jnp.float32), (((1,), (1,)), ((), ())), precision=PRECISE
        )
    )
    grad_first, bc_grad_full, conv_bc_grad, conv_bc_bias_grad = tensor_sum(
        (grad_first_part, bc_part, conv_bc_part, conv_bc_bias_part)
    )
    grad_tokens_norm, norm_gain_grad = first_norm_back(grad_first)
    tokens_grad = (grad_middle + grad_tokens_norm).astype(jnp.bfloat16)
    early = dp_sum((gate_grad, up_grad), (attn_out_grad, mamba_out_grad, down_grad), ())
    late = dp_sum(
        (query_grad, key_grad, value_grad, z_grad, x_grad, bc_grad_full, dt_grad),
        (),
        (
            norm_gain_grad,
            conv_x_grad,
            conv_x_bias_grad,
            conv_bc_grad,
            conv_bc_bias_grad,
            dt_bias_grad,
            a_log_grad,
            skip_grad,
            mixer_gain_grad,
            ffn_gain_grad,
        ),
    )
    matrix_sums = (
        late[0],
        late[1],
        late[2],
        early[2],
        late[3],
        late[4],
        late[5],
        late[6],
        early[3],
        early[0],
        early[1],
        early[4],
    )
    vector_sums = late[7:]
    return (
        block_output,
        tokens_grad,
        vector_sums[0],
        matrix_sums[0],
        matrix_sums[1],
        matrix_sums[2],
        matrix_sums[3],
        matrix_sums[4],
        matrix_sums[5],
        matrix_sums[6],
        matrix_sums[7],
        vector_sums[1],
        vector_sums[2],
        vector_sums[3],
        vector_sums[4],
        vector_sums[5],
        vector_sums[6],
        vector_sums[7],
        vector_sums[8],
        matrix_sums[8],
        vector_sums[9],
        matrix_sums[9],
        matrix_sums[10],
        matrix_sums[11],
    )


def solution(mesh):
    return jax.shard_map(
        body,
        mesh=mesh,
        in_specs=(
            P("dp", None),
            P("dp", None),
            P("dp", None),
            P(),
            P(None, "tensor"),
            P(None, "tensor"),
            P(None, "tensor"),
            P("tensor", None),
            P(None, "tensor"),
            P(None, "tensor"),
            P(),
            P(None, "tensor"),
            P(None, "tensor"),
            P("tensor"),
            P(),
            P(),
            P("tensor"),
            P("tensor"),
            P("tensor"),
            P("tensor"),
            P("tensor", None),
            P(),
            P(None, "tensor"),
            P(None, "tensor"),
            P("tensor", None),
        ),
        out_specs=(
            P("dp", None),
            P("dp", None),
            P(),
            P("dp", "tensor"),
            P("dp", "tensor"),
            P("dp", "tensor"),
            P("tensor", "dp"),
            P("dp", "tensor"),
            P("dp", "tensor"),
            P("dp", None),
            P("dp", "tensor"),
            P(None, "tensor"),
            P("tensor"),
            P(),
            P(),
            P("tensor"),
            P("tensor"),
            P("tensor"),
            P("tensor"),
            P("tensor", "dp"),
            P(),
            P("dp", "tensor"),
            P("dp", "tensor"),
            P("tensor", "dp"),
        ),
        check_vma=False,
    )
```

```python
from functools import partial

import jax
import jax.numpy as jnp
from jax import lax
from jax.sharding import PartitionSpec as P


SSM_HEADS = 24
SSM_HEAD_DIM = 64
STATE = 128
CONV_WIDTH = 4
HEAD_DIM = 64
BLOCK = 128


EPSILON = 1e-05
ROPE_BASE = 100000000000.0
MASKED = -1e30
PRECISE = lax.Precision.HIGHEST


def layout(lengths_row):
    row_count = lengths_row.shape[0] * BLOCK
    block_use = (lengths_row + BLOCK - 1) // BLOCK
    starts = (jnp.cumsum(block_use) - block_use) * BLOCK
    finish = starts + block_use * BLOCK
    slot_ids = jnp.arange(row_count, dtype=jnp.int32)
    inside = (
        (slot_ids[:, None] >= starts[None, :]) & (slot_ids[:, None] < finish[None, :])
    ).astype(jnp.int32)
    seq_start = jnp.sum(inside * starts[None, :], axis=1)
    seq_length = jnp.sum(inside * lengths_row[None, :], axis=1)
    labels = jnp.arange(1, lengths_row.shape[0] + 1, dtype=jnp.int32)
    owners = jnp.sum(inside * labels[None, :], axis=1)
    position = slot_ids - seq_start
    validity = (position < seq_length).astype(jnp.float32)
    carry_on = (position[::BLOCK] != 0).astype(jnp.float32)
    return (position, owners, validity, carry_on)


def project(left, right):
    return jnp.dot(left, right, preferred_element_type=jnp.float32)


def outer_rows(left, right):
    return lax.dot_general(
        left, right, (((0,), (0,)), ((), ())), preferred_element_type=jnp.float32
    )


def back_project(grad_rows, weight):
    return lax.dot_general(
        grad_rows, weight, (((1,), (1,)), ((), ())), preferred_element_type=jnp.float32
    )


def rms_norm(values, gain_vector):
    scaling = lax.rsqrt(jnp.mean(values * values, axis=-1, keepdims=True) + EPSILON)
    return values * scaling * gain_vector


def swiglu(gate_values, up_values):
    return jax.nn.silu(gate_values) * up_values


def rotate(values, position):
    halfway = HEAD_DIM // 2
    frequency = ROPE_BASE ** (-2.0 * jnp.arange(halfway, dtype=jnp.float32) / HEAD_DIM)
    angles = position.astype(jnp.float32)[:, None] * frequency[None, :]
    target_shape = (values.shape[0],) + (1,) * (values.ndim - 2) + (halfway,)
    cosine = jnp.cos(angles).reshape(target_shape)
    sine_part = jnp.sin(angles).reshape(target_shape)
    leading = values[..., :halfway]
    second = values[..., halfway:]
    return jnp.concatenate(
        [leading * cosine - second * sine_part, second * cosine + leading * sine_part], axis=-1
    )


def convolve(values, kernel, offset_terms, position):
    summed = offset_terms[None, :] + kernel[0][None, :] * values
    for shift_by in range(1, CONV_WIDTH):
        earlier = jnp.concatenate(
            [jnp.zeros((shift_by, values.shape[1]), values.dtype), values[:-shift_by]], axis=0
        )
        reached = (position >= shift_by).astype(values.dtype)
        summed = summed + kernel[shift_by][None, :] * earlier * reached[:, None]
    return jax.nn.silu(summed)


def mamba_core(inputs, bc_values, gate_lin, step_lin, step_bias, log_rates, skip_terms, carry_on):
    row_count, head_count = step_lin.shape
    blocks_in = row_count // BLOCK
    step_size = jax.nn.softplus(step_lin + step_bias[None, :])
    decay_rate = -jnp.exp(log_rates)
    streams = inputs.reshape(blocks_in, BLOCK, head_count, SSM_HEAD_DIM)
    write_keys = bc_values[:, :STATE].reshape(blocks_in, BLOCK, STATE)
    read_keys = bc_values[:, STATE:].reshape(blocks_in, BLOCK, STATE)
    steps_in = step_size.reshape(blocks_in, BLOCK, head_count)
    log_decay = jnp.cumsum(steps_in * decay_rate[None, None, :], axis=1)
    causal = jnp.arange(BLOCK)[:, None] >= jnp.arange(BLOCK)[None, :]
    gap_matrix = log_decay[:, :, None, :] - log_decay[:, None, :, :]
    mixing = jnp.exp(jnp.where(causal[None, :, :, None], gap_matrix, MASKED))
    intersection = jnp.einsum("ctn,csn->cts", read_keys, write_keys, precision=PRECISE)
    scaled = streams * steps_in[..., None]
    within = jnp.einsum(
        "ctsh,cshp->cthp", intersection[..., None] * mixing, scaled, precision=PRECISE
    )
    to_end = jnp.exp(log_decay[:, -1:, :] - log_decay)
    pieces = jnp.einsum("csn,cshp->chnp", write_keys, scaled * to_end[..., None], precision=PRECISE)
    decays = jnp.exp(log_decay[:, -1, :])

    def advance(carried, items):
        piece_now, decay_now, keep_now = items
        entering = carried * keep_now
        return (decay_now[:, None, None] * entering + piece_now, entering)

    start_state = jnp.zeros((head_count, STATE, SSM_HEAD_DIM), jnp.float32)
    _, entering = lax.scan(advance, start_state, (pieces, decays, carry_on))
    across = (
        jnp.einsum("ctn,chnp->cthp", read_keys, entering, precision=PRECISE)
        * jnp.exp(log_decay)[..., None]
    )
    result = within + across + skip_terms[None, None, :, None] * streams
    gated = result * jax.nn.silu(gate_lin.reshape(blocks_in, BLOCK, head_count, SSM_HEAD_DIM))
    return gated.reshape(row_count, head_count * SSM_HEAD_DIM)


def block_scores(query_part, key_rows, owners, offset, slot_ids):
    block_rows = query_part.shape[0]
    scores = jnp.einsum(
        "shgd,thd->hgst", query_part, key_rows, preferred_element_type=jnp.float32
    ) * HEAD_DIM ** (-0.5)
    query_ids = offset + jnp.arange(block_rows, dtype=jnp.int32)
    query_owner = lax.dynamic_slice_in_dim(owners, offset, block_rows, 0)
    allowed = (query_owner[:, None] == owners[None, :]) & (slot_ids[None, :] <= query_ids[:, None])
    return jnp.where(allowed, scores, MASKED)


def attend_forward(queries, key_rows, value_rows, owners):
    row_count = queries.shape[0]
    block_rows = min(512, row_count)
    slot_ids = jnp.arange(row_count, dtype=jnp.int32)

    def one_block(offset):
        query_part = lax.dynamic_slice_in_dim(queries, offset, block_rows, 0)
        scores = block_scores(query_part, key_rows, owners, offset, slot_ids)
        maxima = jnp.max(scores, axis=-1, keepdims=True)
        expo = jnp.exp(scores - maxima)
        totals = jnp.sum(expo, axis=-1, keepdims=True)
        probabilities = (expo / totals).astype(jnp.bfloat16)
        result = jnp.einsum(
            "hgst,thd->shgd", probabilities, value_rows, preferred_element_type=jnp.float32
        )
        return (result, (maxima + jnp.log(totals))[..., 0])

    offsets = jnp.arange(0, row_count, block_rows, dtype=jnp.int32)
    results, log_totals = lax.map(one_block, offsets)
    return (results.reshape(queries.shape), log_totals)


def attend_backward(queries, key_rows, value_rows, owners, log_totals, grad_out):
    row_count = queries.shape[0]
    block_rows = min(512, row_count)
    slot_ids = jnp.arange(row_count, dtype=jnp.int32)
    score_scale = HEAD_DIM ** (-0.5)

    def one_block(carried, items):
        key_grad, value_grad = carried
        offset, totals = items
        query_part = lax.dynamic_slice_in_dim(queries, offset, block_rows, 0)
        grad_part = lax.dynamic_slice_in_dim(grad_out, offset, block_rows, 0)
        scores = block_scores(query_part, key_rows, owners, offset, slot_ids)
        probabilities = jnp.exp(scores - totals[..., None])
        value_grad = value_grad + jnp.einsum(
            "hgst,shgd->thd",
            probabilities.astype(jnp.bfloat16),
            grad_part,
            preferred_element_type=jnp.float32,
        )
        prob_grad = jnp.einsum(
            "shgd,thd->hgst", grad_part, value_rows, preferred_element_type=jnp.float32
        )
        score_grad_low = (
            probabilities * (prob_grad - jnp.sum(probabilities * prob_grad, axis=-1, keepdims=True))
        ).astype(jnp.bfloat16)
        query_grad = (
            jnp.einsum(
                "hgst,thd->shgd", score_grad_low, key_rows, preferred_element_type=jnp.float32
            )
            * score_scale
        )
        key_grad = (
            key_grad
            + jnp.einsum(
                "hgst,shgd->thd", score_grad_low, query_part, preferred_element_type=jnp.float32
            )
            * score_scale
        )
        return ((key_grad, value_grad), query_grad)

    offsets = jnp.arange(0, row_count, block_rows, dtype=jnp.int32)
    zeros_kv = jnp.zeros(key_rows.shape, jnp.float32)
    (key_grad, value_grad), query_grads = lax.scan(
        one_block, (zeros_kv, zeros_kv), (offsets, log_totals)
    )
    return (query_grads.reshape(queries.shape), key_grad, value_grad)


def tensor_sum(values):
    if lax.axis_size("tensor") != 2:
        return lax.psum(values, "tensor")
    swapped = lax.ppermute(values, "tensor", perm=[(0, 1), (1, 0)])
    return jax.tree.map(lambda mine, theirs: mine + theirs, values, swapped)


def dp_sum(row_split, col_split, vectors):
    n_dp = lax.axis_size("dp")
    pieces = [g.reshape(n_dp, -1) for g in row_split]
    pieces += [
        g.reshape(g.shape[0], n_dp, g.shape[1] // n_dp).transpose(1, 0, 2).reshape(n_dp, -1)
        for g in col_split
    ]
    pieces += [jnp.broadcast_to(v.reshape(1, -1), (n_dp, v.size)) for v in vectors]
    widths = [p.shape[1] for p in pieces]
    lane_rows = -(-sum(widths) // 16384) * 128
    pieces.append(jnp.zeros((n_dp, lane_rows * 128 - sum(widths)), jnp.float32))
    packed = lax.psum_scatter(
        jnp.concatenate(pieces, axis=1).reshape(n_dp * lane_rows, 128),
        "dp",
        scatter_dimension=0,
        tiled=True,
    ).reshape(-1)
    shapes = [(g.shape[0] // n_dp, g.shape[1]) for g in row_split]
    shapes += [(g.shape[0], g.shape[1] // n_dp) for g in col_split]
    shapes += [v.shape for v in vectors]
    outs = []
    at = 0
    for w, s in zip(widths, shapes):
        outs.append(packed[at : at + w].reshape(s))
        at += w
    return outs


def body(
    tokens,
    cotangent,
    lengths,
    norm_gain,
    query_weight,
    key_weight,
    value_weight,
    attn_out_weight,
    z_weight,
    x_weight,
    bc_weight,
    dt_weight,
    conv_x,
    conv_x_bias,
    conv_bc,
    conv_bc_bias,
    dt_bias,
    a_log,
    skip_gain,
    mixer_gain,
    mamba_out_weight,
    ffn_gain,
    gate_weight,
    up_weight,
    down_weight,
):
    position, owners, validity, carry_on = layout(lengths[0])
    row_count = tokens.shape[0]
    kv_local = key_weight.shape[1] // HEAD_DIM
    grouping = query_weight.shape[1] // key_weight.shape[1]
    group_width = SSM_HEADS * SSM_HEAD_DIM
    valid_col = validity[:, None]
    tokens_wide = tokens.astype(jnp.float32)
    normed, first_norm_back = jax.vjp(rms_norm, tokens_wide, norm_gain)
    first_in = normed.astype(jnp.bfloat16)
    rotation = partial(rotate, position=position)
    query_lin = project(first_in, query_weight).reshape(row_count, kv_local, grouping, HEAD_DIM)
    key_lin = project(first_in, key_weight).reshape(row_count, kv_local, HEAD_DIM)
    value_rows = (
        project(first_in, value_weight).reshape(row_count, kv_local, HEAD_DIM).astype(jnp.bfloat16)
    )
    query_turned, query_unturn = jax.vjp(rotation, query_lin)
    key_turned, key_unturn = jax.vjp(rotation, key_lin)
    queries = query_turned.astype(jnp.bfloat16)
    key_rows = key_turned.astype(jnp.bfloat16)
    attended_wide, log_totals = attend_forward(queries, key_rows, value_rows, owners)
    attended = attended_wide.reshape(row_count, -1).astype(jnp.bfloat16)
    gate_lin = project(first_in, z_weight)
    stream_lin = project(first_in, x_weight)
    bc_lin = project(first_in, bc_weight)
    step_lin = project(first_in, dt_weight)
    causal_filter = partial(convolve, position=position)
    streams_wide, stream_back = jax.vjp(
        causal_filter, stream_lin, conv_x.astype(jnp.float32), conv_x_bias.astype(jnp.float32)
    )
    bc_wide, bc_back = jax.vjp(
        causal_filter, bc_lin, conv_bc.astype(jnp.float32), conv_bc_bias.astype(jnp.float32)
    )
    streams = streams_wide.astype(jnp.bfloat16)
    bc_values = bc_wide.astype(jnp.bfloat16)
    ssm_core = partial(mamba_core, carry_on=carry_on)
    gated_wide, core_back = jax.vjp(
        ssm_core,
        streams.astype(jnp.float32),
        bc_values.astype(jnp.float32),
        gate_lin,
        step_lin,
        dt_bias,
        a_log,
        skip_gain,
    )
    square_sum = lax.psum(jnp.sum(gated_wide * gated_wide, axis=-1), "tensor")
    group_scale = lax.rsqrt(square_sum / group_width + EPSILON)[:, None]
    normed_gated = gated_wide * group_scale
    mixed = (normed_gated * mixer_gain[None, :]).astype(jnp.bfloat16)
    branch_part = project(attended, attn_out_weight) + project(mixed, mamba_out_weight)
    branch = tensor_sum(branch_part)
    middle = tokens_wide + valid_col * branch
    second_wide, second_norm_back = jax.vjp(rms_norm, middle, ffn_gain)
    second_in = second_wide.astype(jnp.bfloat16)
    gate_values = project(second_in, gate_weight)
    up_values = project(second_in, up_weight)
    hidden_wide, hidden_back = jax.vjp(swiglu, gate_values, up_values)
    hidden = hidden_wide.astype(jnp.bfloat16)
    ffn_full = tensor_sum(project(hidden, down_weight))
    cot_wide = cotangent.astype(jnp.float32)
    grad_ffn = (valid_col * cot_wide).astype(jnp.bfloat16)
    down_grad = outer_rows(hidden, grad_ffn)
    grad_hidden = back_project(grad_ffn, down_weight)
    grad_gate_wide, grad_up_wide = hidden_back(grad_hidden)
    grad_gate = grad_gate_wide.astype(jnp.bfloat16)
    grad_up = grad_up_wide.astype(jnp.bfloat16)
    gate_grad = outer_rows(second_in, grad_gate)
    up_grad = outer_rows(second_in, grad_up)
    grad_second = tensor_sum(
        back_project(grad_gate, gate_weight) + back_project(grad_up, up_weight),
    )
    grad_middle_norm, ffn_gain_grad = second_norm_back(grad_second)
    grad_middle = cot_wide + grad_middle_norm
    grad_branch = (valid_col * grad_middle).astype(jnp.bfloat16)
    attn_out_grad = outer_rows(attended, grad_branch)
    mamba_out_grad = outer_rows(mixed, grad_branch)
    grad_attended = (
        back_project(grad_branch, attn_out_weight)
        .astype(jnp.bfloat16)
        .reshape(row_count, kv_local, grouping, HEAD_DIM)
    )
    grad_mixed = back_project(grad_branch, mamba_out_weight)
    gain_scaled = grad_mixed * mixer_gain[None, :]
    mixer_gain_grad = jnp.sum(grad_mixed * normed_gated, axis=0)
    cross_sum = lax.psum(jnp.sum(gain_scaled * normed_gated, axis=-1), "tensor")
    grad_gated = group_scale * (gain_scaled - normed_gated * (cross_sum / group_width)[:, None])
    grad_streams, grad_bc, grad_gate_lin, grad_step_lin, dt_bias_grad, a_log_grad, skip_grad = (
        core_back(grad_gated)
    )
    grad_stream_lin, conv_x_grad, conv_x_bias_grad = stream_back(grad_streams)
    grad_bc_lin, conv_bc_part, conv_bc_bias_part = bc_back(grad_bc)
    grad_query, grad_key, grad_value = attend_backward(
        queries, key_rows, value_rows, owners, log_totals, grad_attended
    )
    (grad_query_lin,) = query_unturn(grad_query)
    (grad_key_lin,) = key_unturn(grad_key)
    grad_query_low = grad_query_lin.reshape(row_count, -1).astype(jnp.bfloat16)
    grad_key_low = grad_key_lin.reshape(row_count, -1).astype(jnp.bfloat16)
    grad_value_low = grad_value.reshape(row_count, -1).astype(jnp.bfloat16)
    grad_gate_low = grad_gate_lin.astype(jnp.bfloat16)
    grad_stream_low = grad_stream_lin.astype(jnp.bfloat16)
    grad_step_low = grad_step_lin.astype(jnp.bfloat16)
    query_grad = outer_rows(first_in, grad_query_low)
    key_grad = outer_rows(first_in, grad_key_low)
    value_grad = outer_rows(first_in, grad_value_low)
    z_grad = outer_rows(first_in, grad_gate_low)
    x_grad = outer_rows(first_in, grad_stream_low)
    dt_grad = outer_rows(first_in, grad_step_low)
    bc_part = lax.dot_general(
        first_in.astype(jnp.float32), grad_bc_lin, (((0,), (0,)), ((), ())), precision=PRECISE
    )
    grad_first_part = (
        back_project(grad_query_low, query_weight)
        + back_project(grad_key_low, key_weight)
        + back_project(grad_value_low, value_weight)
        + back_project(grad_gate_low, z_weight)
        + back_project(grad_stream_low, x_weight)
        + back_project(grad_step_low, dt_weight)
        + lax.dot_general(
            grad_bc_lin, bc_weight.astype(jnp.float32), (((1,), (1,)), ((), ())), precision=PRECISE
        )
    )
    grad_first, bc_grad_full, conv_bc_grad, conv_bc_bias_grad = tensor_sum(
        (grad_first_part, bc_part, conv_bc_part, conv_bc_bias_part)
    )
    grad_tokens_norm, norm_gain_grad = first_norm_back(grad_first)
    ffn_late, middle_late, _ = lax.optimization_barrier((ffn_full, middle, grad_first))
    block_output = (middle_late + valid_col * ffn_late).astype(jnp.bfloat16)
    tokens_grad = (grad_middle + grad_tokens_norm).astype(jnp.bfloat16)
    early = dp_sum((gate_grad, up_grad), (attn_out_grad, mamba_out_grad, down_grad), ())
    late = dp_sum(
        (query_grad, key_grad, value_grad, z_grad, x_grad, bc_grad_full, dt_grad),
        (),
        (
            norm_gain_grad,
            conv_x_grad,
            conv_x_bias_grad,
            conv_bc_grad,
            conv_bc_bias_grad,
            dt_bias_grad,
            a_log_grad,
            skip_grad,
            mixer_gain_grad,
            ffn_gain_grad,
        ),
    )
    matrix_sums = (
        late[0],
        late[1],
        late[2],
        early[2],
        late[3],
        late[4],
        late[5],
        late[6],
        early[3],
        early[0],
        early[1],
        early[4],
    )
    vector_sums = late[7:]
    return (
        block_output,
        tokens_grad,
        vector_sums[0],
        matrix_sums[0],
        matrix_sums[1],
        matrix_sums[2],
        matrix_sums[3],
        matrix_sums[4],
        matrix_sums[5],
        matrix_sums[6],
        matrix_sums[7],
        vector_sums[1],
        vector_sums[2],
        vector_sums[3],
        vector_sums[4],
        vector_sums[5],
        vector_sums[6],
        vector_sums[7],
        vector_sums[8],
        matrix_sums[8],
        vector_sums[9],
        matrix_sums[9],
        matrix_sums[10],
        matrix_sums[11],
    )


def solution(mesh):
    return jax.shard_map(
        body,
        mesh=mesh,
        in_specs=(
            P("dp", None),
            P("dp", None),
            P("dp", None),
            P(),
            P(None, "tensor"),
            P(None, "tensor"),
            P(None, "tensor"),
            P("tensor", None),
            P(None, "tensor"),
            P(None, "tensor"),
            P(),
            P(None, "tensor"),
            P(None, "tensor"),
            P("tensor"),
            P(),
            P(),
            P("tensor"),
            P("tensor"),
            P("tensor"),
            P("tensor"),
            P("tensor", None),
            P(),
            P(None, "tensor"),
            P(None, "tensor"),
            P("tensor", None),
        ),
        out_specs=(
            P("dp", None),
            P("dp", None),
            P(),
            P("dp", "tensor"),
            P("dp", "tensor"),
            P("dp", "tensor"),
            P("tensor", "dp"),
            P("dp", "tensor"),
            P("dp", "tensor"),
            P("dp", None),
            P("dp", "tensor"),
            P(None, "tensor"),
            P("tensor"),
            P(),
            P(),
            P("tensor"),
            P("tensor"),
            P("tensor"),
            P("tensor"),
            P("tensor", "dp"),
            P(),
            P("dp", "tensor"),
            P("dp", "tensor"),
            P("tensor", "dp"),
        ),
        check_vma=False,
    )
```

```python
from functools import partial

import jax
import jax.numpy as jnp
from jax import lax
from jax.sharding import PartitionSpec as P


SSM_HEADS = 24
SSM_HEAD_DIM = 64
STATE = 128
CONV_WIDTH = 4
HEAD_DIM = 64
BLOCK = 128


EPSILON = 1e-05
ROPE_BASE = 100000000000.0
MASKED = -1e30
PRECISE = lax.Precision.HIGHEST


def layout(lengths_row):
    row_count = lengths_row.shape[0] * BLOCK
    block_use = (lengths_row + BLOCK - 1) // BLOCK
    starts = (jnp.cumsum(block_use) - block_use) * BLOCK
    finish = starts + block_use * BLOCK
    slot_ids = jnp.arange(row_count, dtype=jnp.int32)
    inside = (
        (slot_ids[:, None] >= starts[None, :]) & (slot_ids[:, None] < finish[None, :])
    ).astype(jnp.int32)
    seq_start = jnp.sum(inside * starts[None, :], axis=1)
    seq_length = jnp.sum(inside * lengths_row[None, :], axis=1)
    labels = jnp.arange(1, lengths_row.shape[0] + 1, dtype=jnp.int32)
    owners = jnp.sum(inside * labels[None, :], axis=1)
    position = slot_ids - seq_start
    validity = (position < seq_length).astype(jnp.float32)
    carry_on = (position[::BLOCK] != 0).astype(jnp.float32)
    return (position, owners, validity, carry_on)


def project(left, right):
    return jnp.dot(left, right, preferred_element_type=jnp.float32)


def outer_rows(left, right):
    return lax.dot_general(
        left, right, (((0,), (0,)), ((), ())), preferred_element_type=jnp.float32
    )


def back_project(grad_rows, weight):
    return lax.dot_general(
        grad_rows, weight, (((1,), (1,)), ((), ())), preferred_element_type=jnp.float32
    )


def rms_norm(values, gain_vector):
    scaling = lax.rsqrt(jnp.mean(values * values, axis=-1, keepdims=True) + EPSILON)
    return values * scaling * gain_vector


def swiglu(gate_values, up_values):
    return jax.nn.silu(gate_values) * up_values


def rotate(values, position):
    halfway = HEAD_DIM // 2
    frequency = ROPE_BASE ** (-2.0 * jnp.arange(halfway, dtype=jnp.float32) / HEAD_DIM)
    angles = position.astype(jnp.float32)[:, None] * frequency[None, :]
    target_shape = (values.shape[0],) + (1,) * (values.ndim - 2) + (halfway,)
    cosine = jnp.cos(angles).reshape(target_shape)
    sine_part = jnp.sin(angles).reshape(target_shape)
    leading = values[..., :halfway]
    second = values[..., halfway:]
    return jnp.concatenate(
        [leading * cosine - second * sine_part, second * cosine + leading * sine_part], axis=-1
    )


def convolve(values, kernel, offset_terms, position):
    summed = offset_terms[None, :] + kernel[0][None, :] * values
    for shift_by in range(1, CONV_WIDTH):
        earlier = jnp.concatenate(
            [jnp.zeros((shift_by, values.shape[1]), values.dtype), values[:-shift_by]], axis=0
        )
        reached = (position >= shift_by).astype(values.dtype)
        summed = summed + kernel[shift_by][None, :] * earlier * reached[:, None]
    return jax.nn.silu(summed)


def mamba_core(inputs, bc_values, gate_lin, step_lin, step_bias, log_rates, skip_terms, carry_on):
    row_count, head_count = step_lin.shape
    blocks_in = row_count // BLOCK
    step_size = jax.nn.softplus(step_lin + step_bias[None, :])
    decay_rate = -jnp.exp(log_rates)
    streams = inputs.reshape(blocks_in, BLOCK, head_count, SSM_HEAD_DIM)
    write_keys = bc_values[:, :STATE].reshape(blocks_in, BLOCK, STATE)
    read_keys = bc_values[:, STATE:].reshape(blocks_in, BLOCK, STATE)
    steps_in = step_size.reshape(blocks_in, BLOCK, head_count)
    log_decay = jnp.cumsum(steps_in * decay_rate[None, None, :], axis=1)
    causal = jnp.arange(BLOCK)[:, None] >= jnp.arange(BLOCK)[None, :]
    gap_matrix = log_decay[:, :, None, :] - log_decay[:, None, :, :]
    mixing = jnp.exp(jnp.where(causal[None, :, :, None], gap_matrix, MASKED))
    intersection = jnp.einsum("ctn,csn->cts", read_keys, write_keys, precision=PRECISE)
    scaled = streams * steps_in[..., None]
    within = jnp.einsum(
        "ctsh,cshp->cthp", intersection[..., None] * mixing, scaled, precision=PRECISE
    )
    to_end = jnp.exp(log_decay[:, -1:, :] - log_decay)
    pieces = jnp.einsum("csn,cshp->chnp", write_keys, scaled * to_end[..., None], precision=PRECISE)
    decays = jnp.exp(log_decay[:, -1, :])

    def advance(carried, items):
        piece_now, decay_now, keep_now = items
        entering = carried * keep_now
        return (decay_now[:, None, None] * entering + piece_now, entering)

    start_state = jnp.zeros((head_count, STATE, SSM_HEAD_DIM), jnp.float32)
    _, entering = lax.scan(advance, start_state, (pieces, decays, carry_on))
    across = (
        jnp.einsum("ctn,chnp->cthp", read_keys, entering, precision=PRECISE)
        * jnp.exp(log_decay)[..., None]
    )
    result = within + across + skip_terms[None, None, :, None] * streams
    gated = result * jax.nn.silu(gate_lin.reshape(blocks_in, BLOCK, head_count, SSM_HEAD_DIM))
    return gated.reshape(row_count, head_count * SSM_HEAD_DIM)


def block_scores(query_part, key_rows, owners, offset, slot_ids):
    block_rows = query_part.shape[0]
    scores = jnp.einsum(
        "shgd,thd->hgst", query_part, key_rows, preferred_element_type=jnp.float32
    ) * HEAD_DIM ** (-0.5)
    query_ids = offset + jnp.arange(block_rows, dtype=jnp.int32)
    query_owner = lax.dynamic_slice_in_dim(owners, offset, block_rows, 0)
    allowed = (query_owner[:, None] == owners[None, :]) & (slot_ids[None, :] <= query_ids[:, None])
    return jnp.where(allowed, scores, MASKED)


def attend_forward(queries, key_rows, value_rows, owners):
    row_count = queries.shape[0]
    block_rows = min(512, row_count)
    slot_ids = jnp.arange(row_count, dtype=jnp.int32)

    def one_block(offset):
        query_part = lax.dynamic_slice_in_dim(queries, offset, block_rows, 0)
        scores = block_scores(query_part, key_rows, owners, offset, slot_ids)
        maxima = jnp.max(scores, axis=-1, keepdims=True)
        expo = jnp.exp(scores - maxima)
        totals = jnp.sum(expo, axis=-1, keepdims=True)
        probabilities = (expo / totals).astype(jnp.bfloat16)
        result = jnp.einsum(
            "hgst,thd->shgd", probabilities, value_rows, preferred_element_type=jnp.float32
        )
        return (result, (maxima + jnp.log(totals))[..., 0])

    offsets = jnp.arange(0, row_count, block_rows, dtype=jnp.int32)
    results, log_totals = lax.map(one_block, offsets)
    return (results.reshape(queries.shape), log_totals)


def attend_backward(queries, key_rows, value_rows, owners, log_totals, grad_out):
    row_count = queries.shape[0]
    block_rows = min(512, row_count)
    slot_ids = jnp.arange(row_count, dtype=jnp.int32)
    score_scale = HEAD_DIM ** (-0.5)

    def one_block(carried, items):
        key_grad, value_grad = carried
        offset, totals = items
        query_part = lax.dynamic_slice_in_dim(queries, offset, block_rows, 0)
        grad_part = lax.dynamic_slice_in_dim(grad_out, offset, block_rows, 0)
        scores = block_scores(query_part, key_rows, owners, offset, slot_ids)
        probabilities = jnp.exp(scores - totals[..., None])
        value_grad = value_grad + jnp.einsum(
            "hgst,shgd->thd",
            probabilities.astype(jnp.bfloat16),
            grad_part,
            preferred_element_type=jnp.float32,
        )
        prob_grad = jnp.einsum(
            "shgd,thd->hgst", grad_part, value_rows, preferred_element_type=jnp.float32
        )
        score_grad_low = (
            probabilities * (prob_grad - jnp.sum(probabilities * prob_grad, axis=-1, keepdims=True))
        ).astype(jnp.bfloat16)
        query_grad = (
            jnp.einsum(
                "hgst,thd->shgd", score_grad_low, key_rows, preferred_element_type=jnp.float32
            )
            * score_scale
        )
        key_grad = (
            key_grad
            + jnp.einsum(
                "hgst,shgd->thd", score_grad_low, query_part, preferred_element_type=jnp.float32
            )
            * score_scale
        )
        return ((key_grad, value_grad), query_grad)

    offsets = jnp.arange(0, row_count, block_rows, dtype=jnp.int32)
    zeros_kv = jnp.zeros(key_rows.shape, jnp.float32)
    (key_grad, value_grad), query_grads = lax.scan(
        one_block, (zeros_kv, zeros_kv), (offsets, log_totals)
    )
    return (query_grads.reshape(queries.shape), key_grad, value_grad)


def tensor_sum(values):
    if lax.axis_size("tensor") != 2:
        return lax.psum(values, "tensor")
    swapped = lax.ppermute(values, "tensor", perm=[(0, 1), (1, 0)])
    return jax.tree.map(lambda mine, theirs: mine + theirs, values, swapped)


def dp_sum(row_split, col_split, vectors):
    n_dp = lax.axis_size("dp")
    pieces = [g.reshape(n_dp, -1) for g in row_split]
    pieces += [
        g.reshape(g.shape[0], n_dp, g.shape[1] // n_dp).transpose(1, 0, 2).reshape(n_dp, -1)
        for g in col_split
    ]
    pieces += [jnp.broadcast_to(v.reshape(1, -1), (n_dp, v.size)) for v in vectors]
    widths = [p.shape[1] for p in pieces]
    lane_rows = -(-sum(widths) // 16384) * 128
    pieces.append(jnp.zeros((n_dp, lane_rows * 128 - sum(widths)), jnp.float32))
    packed = lax.psum_scatter(
        jnp.concatenate(pieces, axis=1).reshape(n_dp * lane_rows, 128),
        "dp",
        scatter_dimension=0,
        tiled=True,
    ).reshape(-1)
    shapes = [(g.shape[0] // n_dp, g.shape[1]) for g in row_split]
    shapes += [(g.shape[0], g.shape[1] // n_dp) for g in col_split]
    shapes += [v.shape for v in vectors]
    outs = []
    at = 0
    for w, s in zip(widths, shapes):
        outs.append(packed[at : at + w].reshape(s))
        at += w
    return outs


def body(
    tokens,
    cotangent,
    lengths,
    norm_gain,
    query_weight,
    key_weight,
    value_weight,
    attn_out_weight,
    z_weight,
    x_weight,
    bc_weight,
    dt_weight,
    conv_x,
    conv_x_bias,
    conv_bc,
    conv_bc_bias,
    dt_bias,
    a_log,
    skip_gain,
    mixer_gain,
    mamba_out_weight,
    ffn_gain,
    gate_weight,
    up_weight,
    down_weight,
):
    position, owners, validity, carry_on = layout(lengths[0])
    row_count = tokens.shape[0]
    kv_local = key_weight.shape[1] // HEAD_DIM
    grouping = query_weight.shape[1] // key_weight.shape[1]
    group_width = SSM_HEADS * SSM_HEAD_DIM
    valid_col = validity[:, None]
    tokens_wide = tokens.astype(jnp.float32)
    normed, first_norm_back = jax.vjp(rms_norm, tokens_wide, norm_gain)
    first_in = normed.astype(jnp.bfloat16)
    rotation = partial(rotate, position=position)
    query_lin = project(first_in, query_weight).reshape(row_count, kv_local, grouping, HEAD_DIM)
    key_lin = project(first_in, key_weight).reshape(row_count, kv_local, HEAD_DIM)
    value_rows = (
        project(first_in, value_weight).reshape(row_count, kv_local, HEAD_DIM).astype(jnp.bfloat16)
    )
    query_turned, query_unturn = jax.vjp(rotation, query_lin)
    key_turned, key_unturn = jax.vjp(rotation, key_lin)
    queries = query_turned.astype(jnp.bfloat16)
    key_rows = key_turned.astype(jnp.bfloat16)
    attended_wide, log_totals = attend_forward(queries, key_rows, value_rows, owners)
    attended = attended_wide.reshape(row_count, -1).astype(jnp.bfloat16)
    gate_lin = project(first_in, z_weight)
    stream_lin = project(first_in, x_weight)
    bc_lin = project(first_in, bc_weight)
    step_lin = project(first_in, dt_weight)
    causal_filter = partial(convolve, position=position)
    streams_wide, stream_back = jax.vjp(
        causal_filter, stream_lin, conv_x.astype(jnp.float32), conv_x_bias.astype(jnp.float32)
    )
    bc_wide, bc_back = jax.vjp(
        causal_filter, bc_lin, conv_bc.astype(jnp.float32), conv_bc_bias.astype(jnp.float32)
    )
    streams = streams_wide.astype(jnp.bfloat16)
    bc_values = bc_wide.astype(jnp.bfloat16)
    ssm_core = partial(mamba_core, carry_on=carry_on)
    gated_wide, core_back = jax.vjp(
        ssm_core,
        streams.astype(jnp.float32),
        bc_values.astype(jnp.float32),
        gate_lin,
        step_lin,
        dt_bias,
        a_log,
        skip_gain,
    )
    square_sum = lax.psum(jnp.sum(gated_wide * gated_wide, axis=-1), "tensor")
    group_scale = lax.rsqrt(square_sum / group_width + EPSILON)[:, None]
    normed_gated = gated_wide * group_scale
    mixed = (normed_gated * mixer_gain[None, :]).astype(jnp.bfloat16)
    branch_part = project(attended, attn_out_weight) + project(mixed, mamba_out_weight)
    branch = tensor_sum(branch_part)
    middle = tokens_wide + valid_col * branch
    second_wide, second_norm_back = jax.vjp(rms_norm, middle, ffn_gain)
    second_in = second_wide.astype(jnp.bfloat16)
    gate_values = project(second_in, gate_weight)
    up_values = project(second_in, up_weight)
    hidden_wide, hidden_back = jax.vjp(swiglu, gate_values, up_values)
    hidden = hidden_wide.astype(jnp.bfloat16)
    ffn_full = tensor_sum(project(hidden, down_weight))
    cot_wide = cotangent.astype(jnp.float32)
    grad_ffn = (valid_col * cot_wide).astype(jnp.bfloat16)
    down_grad = outer_rows(hidden, grad_ffn)
    grad_hidden = back_project(grad_ffn, down_weight)
    grad_gate_wide, grad_up_wide = hidden_back(grad_hidden)
    grad_gate = grad_gate_wide.astype(jnp.bfloat16)
    grad_up = grad_up_wide.astype(jnp.bfloat16)
    gate_grad = outer_rows(second_in, grad_gate)
    up_grad = outer_rows(second_in, grad_up)
    grad_second = tensor_sum(
        back_project(grad_gate, gate_weight) + back_project(grad_up, up_weight),
    )
    grad_middle_norm, ffn_gain_grad = second_norm_back(grad_second)
    grad_middle = cot_wide + grad_middle_norm
    grad_branch = (valid_col * grad_middle).astype(jnp.bfloat16)
    attn_out_grad = outer_rows(attended, grad_branch)
    mamba_out_grad = outer_rows(mixed, grad_branch)
    grad_attended = (
        back_project(grad_branch, attn_out_weight)
        .astype(jnp.bfloat16)
        .reshape(row_count, kv_local, grouping, HEAD_DIM)
    )
    grad_mixed = back_project(grad_branch, mamba_out_weight)
    gain_scaled = grad_mixed * mixer_gain[None, :]
    mixer_gain_grad = jnp.sum(grad_mixed * normed_gated, axis=0)
    cross_sum = lax.psum(jnp.sum(gain_scaled * normed_gated, axis=-1), "tensor")
    grad_gated = group_scale * (gain_scaled - normed_gated * (cross_sum / group_width)[:, None])
    grad_streams, grad_bc, grad_gate_lin, grad_step_lin, dt_bias_grad, a_log_grad, skip_grad = (
        core_back(grad_gated)
    )
    grad_stream_lin, conv_x_grad, conv_x_bias_grad = stream_back(grad_streams)
    grad_bc_lin, conv_bc_part, conv_bc_bias_part = bc_back(grad_bc)
    grad_query, grad_key, grad_value = attend_backward(
        queries, key_rows, value_rows, owners, log_totals, grad_attended
    )
    (grad_query_lin,) = query_unturn(grad_query)
    (grad_key_lin,) = key_unturn(grad_key)
    grad_query_low = grad_query_lin.reshape(row_count, -1).astype(jnp.bfloat16)
    grad_key_low = grad_key_lin.reshape(row_count, -1).astype(jnp.bfloat16)
    grad_value_low = grad_value.reshape(row_count, -1).astype(jnp.bfloat16)
    grad_gate_low = grad_gate_lin.astype(jnp.bfloat16)
    grad_stream_low = grad_stream_lin.astype(jnp.bfloat16)
    grad_step_low = grad_step_lin.astype(jnp.bfloat16)
    query_grad = outer_rows(first_in, grad_query_low)
    key_grad = outer_rows(first_in, grad_key_low)
    value_grad = outer_rows(first_in, grad_value_low)
    z_grad = outer_rows(first_in, grad_gate_low)
    x_grad = outer_rows(first_in, grad_stream_low)
    dt_grad = outer_rows(first_in, grad_step_low)
    bc_part = lax.dot_general(
        first_in.astype(jnp.float32), grad_bc_lin, (((0,), (0,)), ((), ())), precision=PRECISE
    )
    grad_first_part = (
        back_project(grad_query_low, query_weight)
        + back_project(grad_key_low, key_weight)
        + back_project(grad_value_low, value_weight)
        + back_project(grad_gate_low, z_weight)
        + back_project(grad_stream_low, x_weight)
        + back_project(grad_step_low, dt_weight)
        + lax.dot_general(
            grad_bc_lin, bc_weight.astype(jnp.float32), (((1,), (1,)), ((), ())), precision=PRECISE
        )
    )
    first_scale = lax.rsqrt(jnp.mean(tokens_wide * tokens_wide, axis=-1, keepdims=True) + EPSILON)
    norm_gain_part = jnp.sum(grad_first_part * (tokens_wide * first_scale), axis=0)
    grad_first_part, norm_gain_part = lax.optimization_barrier((grad_first_part, norm_gain_part))
    grad_first = tensor_sum(grad_first_part)
    grad_tokens_norm, _ = first_norm_back(grad_first)
    ffn_late, middle_late, _ = lax.optimization_barrier((ffn_full, middle, grad_first))
    block_output = (middle_late + valid_col * ffn_late).astype(jnp.bfloat16)
    tokens_grad = (grad_middle + grad_tokens_norm).astype(jnp.bfloat16)
    early = dp_sum((gate_grad, up_grad), (attn_out_grad, mamba_out_grad, down_grad), ())
    late = dp_sum(
        (query_grad, key_grad, value_grad, z_grad, x_grad, bc_part, dt_grad),
        (),
        (
            norm_gain_part,
            conv_x_grad,
            conv_x_bias_grad,
            conv_bc_part,
            conv_bc_bias_part,
            dt_bias_grad,
            a_log_grad,
            skip_grad,
            mixer_gain_grad,
            ffn_gain_grad,
        ),
    )
    late = list(late)
    late[5], late[7], late[10], late[11] = tensor_sum((late[5], late[7], late[10], late[11]))
    matrix_sums = (
        late[0],
        late[1],
        late[2],
        early[2],
        late[3],
        late[4],
        late[5],
        late[6],
        early[3],
        early[0],
        early[1],
        early[4],
    )
    vector_sums = late[7:]
    return (
        block_output,
        tokens_grad,
        vector_sums[0],
        matrix_sums[0],
        matrix_sums[1],
        matrix_sums[2],
        matrix_sums[3],
        matrix_sums[4],
        matrix_sums[5],
        matrix_sums[6],
        matrix_sums[7],
        vector_sums[1],
        vector_sums[2],
        vector_sums[3],
        vector_sums[4],
        vector_sums[5],
        vector_sums[6],
        vector_sums[7],
        vector_sums[8],
        matrix_sums[8],
        vector_sums[9],
        matrix_sums[9],
        matrix_sums[10],
        matrix_sums[11],
    )


def solution(mesh):
    return jax.shard_map(
        body,
        mesh=mesh,
        in_specs=(
            P("dp", None),
            P("dp", None),
            P("dp", None),
            P(),
            P(None, "tensor"),
            P(None, "tensor"),
            P(None, "tensor"),
            P("tensor", None),
            P(None, "tensor"),
            P(None, "tensor"),
            P(),
            P(None, "tensor"),
            P(None, "tensor"),
            P("tensor"),
            P(),
            P(),
            P("tensor"),
            P("tensor"),
            P("tensor"),
            P("tensor"),
            P("tensor", None),
            P(),
            P(None, "tensor"),
            P(None, "tensor"),
            P("tensor", None),
        ),
        out_specs=(
            P("dp", None),
            P("dp", None),
            P(),
            P("dp", "tensor"),
            P("dp", "tensor"),
            P("dp", "tensor"),
            P("tensor", "dp"),
            P("dp", "tensor"),
            P("dp", "tensor"),
            P("dp", None),
            P("dp", "tensor"),
            P(None, "tensor"),
            P("tensor"),
            P(),
            P(),
            P("tensor"),
            P("tensor"),
            P("tensor"),
            P("tensor"),
            P("tensor", "dp"),
            P(),
            P("dp", "tensor"),
            P("dp", "tensor"),
            P("tensor", "dp"),
        ),
        check_vma=False,
    )
```

```python
from functools import partial

import jax
import jax.numpy as jnp
from jax import lax
from jax.sharding import PartitionSpec as P


SSM_HEADS = 24
SSM_HEAD_DIM = 64
STATE = 128
CONV_WIDTH = 4
HEAD_DIM = 64
BLOCK = 128


EPSILON = 1e-05
ROPE_BASE = 100000000000.0
MASKED = -1e30
PRECISE = lax.Precision.HIGHEST


def layout(lengths_row):
    row_count = lengths_row.shape[0] * BLOCK
    block_use = (lengths_row + BLOCK - 1) // BLOCK
    starts = (jnp.cumsum(block_use) - block_use) * BLOCK
    finish = starts + block_use * BLOCK
    slot_ids = jnp.arange(row_count, dtype=jnp.int32)
    inside = (
        (slot_ids[:, None] >= starts[None, :]) & (slot_ids[:, None] < finish[None, :])
    ).astype(jnp.int32)
    seq_start = jnp.sum(inside * starts[None, :], axis=1)
    seq_length = jnp.sum(inside * lengths_row[None, :], axis=1)
    labels = jnp.arange(1, lengths_row.shape[0] + 1, dtype=jnp.int32)
    owners = jnp.sum(inside * labels[None, :], axis=1)
    position = slot_ids - seq_start
    validity = (position < seq_length).astype(jnp.float32)
    carry_on = (position[::BLOCK] != 0).astype(jnp.float32)
    return (position, owners, validity, carry_on)


def project(left, right):
    return jnp.dot(left, right, preferred_element_type=jnp.float32)


def outer_rows(left, right):
    return lax.dot_general(
        left, right, (((0,), (0,)), ((), ())), preferred_element_type=jnp.float32
    )


def back_project(grad_rows, weight):
    return lax.dot_general(
        grad_rows, weight, (((1,), (1,)), ((), ())), preferred_element_type=jnp.float32
    )


def rms_norm(values, gain_vector):
    scaling = lax.rsqrt(jnp.mean(values * values, axis=-1, keepdims=True) + EPSILON)
    return values * scaling * gain_vector


def swiglu(gate_values, up_values):
    return jax.nn.silu(gate_values) * up_values


def rotate(values, position):
    halfway = HEAD_DIM // 2
    frequency = ROPE_BASE ** (-2.0 * jnp.arange(halfway, dtype=jnp.float32) / HEAD_DIM)
    angles = position.astype(jnp.float32)[:, None] * frequency[None, :]
    target_shape = (values.shape[0],) + (1,) * (values.ndim - 2) + (halfway,)
    cosine = jnp.cos(angles).reshape(target_shape)
    sine_part = jnp.sin(angles).reshape(target_shape)
    leading = values[..., :halfway]
    second = values[..., halfway:]
    return jnp.concatenate(
        [leading * cosine - second * sine_part, second * cosine + leading * sine_part], axis=-1
    )


def convolve(values, kernel, offset_terms, position):
    summed = offset_terms[None, :] + kernel[0][None, :] * values
    for shift_by in range(1, CONV_WIDTH):
        earlier = jnp.concatenate(
            [jnp.zeros((shift_by, values.shape[1]), values.dtype), values[:-shift_by]], axis=0
        )
        reached = (position >= shift_by).astype(values.dtype)
        summed = summed + kernel[shift_by][None, :] * earlier * reached[:, None]
    return jax.nn.silu(summed)


def mamba_core(inputs, bc_values, gate_lin, step_lin, step_bias, log_rates, skip_terms, carry_on):
    row_count, head_count = step_lin.shape
    blocks_in = row_count // BLOCK
    step_size = jax.nn.softplus(step_lin + step_bias[None, :])
    decay_rate = -jnp.exp(log_rates)
    streams = inputs.reshape(blocks_in, BLOCK, head_count, SSM_HEAD_DIM)
    write_keys = bc_values[:, :STATE].reshape(blocks_in, BLOCK, STATE)
    read_keys = bc_values[:, STATE:].reshape(blocks_in, BLOCK, STATE)
    steps_in = step_size.reshape(blocks_in, BLOCK, head_count)
    log_decay = jnp.cumsum(steps_in * decay_rate[None, None, :], axis=1)
    causal = jnp.arange(BLOCK)[:, None] >= jnp.arange(BLOCK)[None, :]
    gap_matrix = log_decay[:, :, None, :] - log_decay[:, None, :, :]
    mixing = jnp.exp(jnp.where(causal[None, :, :, None], gap_matrix, MASKED))
    intersection = jnp.einsum("ctn,csn->cts", read_keys, write_keys, precision=PRECISE)
    scaled = streams * steps_in[..., None]
    within = jnp.einsum(
        "ctsh,cshp->cthp", intersection[..., None] * mixing, scaled, precision=PRECISE
    )
    to_end = jnp.exp(log_decay[:, -1:, :] - log_decay)
    pieces = jnp.einsum("csn,cshp->chnp", write_keys, scaled * to_end[..., None], precision=PRECISE)
    decays = jnp.exp(log_decay[:, -1, :])

    def advance(carried, items):
        piece_now, decay_now, keep_now = items
        entering = carried * keep_now
        return (decay_now[:, None, None] * entering + piece_now, entering)

    start_state = jnp.zeros((head_count, STATE, SSM_HEAD_DIM), jnp.float32)
    _, entering = lax.scan(advance, start_state, (pieces, decays, carry_on))
    across = (
        jnp.einsum("ctn,chnp->cthp", read_keys, entering, precision=PRECISE)
        * jnp.exp(log_decay)[..., None]
    )
    result = within + across + skip_terms[None, None, :, None] * streams
    gated = result * jax.nn.silu(gate_lin.reshape(blocks_in, BLOCK, head_count, SSM_HEAD_DIM))
    return gated.reshape(row_count, head_count * SSM_HEAD_DIM)


def block_scores(query_part, key_rows, owners, offset, slot_ids):
    block_rows = query_part.shape[0]
    scores = jnp.einsum(
        "shgd,thd->hgst", query_part, key_rows, preferred_element_type=jnp.float32
    ) * HEAD_DIM ** (-0.5)
    query_ids = offset + jnp.arange(block_rows, dtype=jnp.int32)
    query_owner = lax.dynamic_slice_in_dim(owners, offset, block_rows, 0)
    allowed = (query_owner[:, None] == owners[None, :]) & (slot_ids[None, :] <= query_ids[:, None])
    return jnp.where(allowed, scores, MASKED)


def attend_forward(queries, key_rows, value_rows, owners):
    row_count = queries.shape[0]
    block_rows = min(512, row_count)
    slot_ids = jnp.arange(row_count, dtype=jnp.int32)

    def one_block(offset):
        query_part = lax.dynamic_slice_in_dim(queries, offset, block_rows, 0)
        scores = block_scores(query_part, key_rows, owners, offset, slot_ids)
        maxima = jnp.max(scores, axis=-1, keepdims=True)
        expo = jnp.exp(scores - maxima)
        totals = jnp.sum(expo, axis=-1, keepdims=True)
        probabilities = (expo / totals).astype(jnp.bfloat16)
        result = jnp.einsum(
            "hgst,thd->shgd", probabilities, value_rows, preferred_element_type=jnp.float32
        )
        return (result, (maxima + jnp.log(totals))[..., 0])

    offsets = jnp.arange(0, row_count, block_rows, dtype=jnp.int32)
    results, log_totals = lax.map(one_block, offsets)
    return (results.reshape(queries.shape), log_totals)


def attend_backward(queries, key_rows, value_rows, owners, log_totals, grad_out):
    row_count = queries.shape[0]
    block_rows = min(512, row_count)
    slot_ids = jnp.arange(row_count, dtype=jnp.int32)
    score_scale = HEAD_DIM ** (-0.5)

    def one_block(carried, items):
        key_grad, value_grad = carried
        offset, totals = items
        query_part = lax.dynamic_slice_in_dim(queries, offset, block_rows, 0)
        grad_part = lax.dynamic_slice_in_dim(grad_out, offset, block_rows, 0)
        scores = block_scores(query_part, key_rows, owners, offset, slot_ids)
        probabilities = jnp.exp(scores - totals[..., None])
        value_grad = value_grad + jnp.einsum(
            "hgst,shgd->thd",
            probabilities.astype(jnp.bfloat16),
            grad_part,
            preferred_element_type=jnp.float32,
        )
        prob_grad = jnp.einsum(
            "shgd,thd->hgst", grad_part, value_rows, preferred_element_type=jnp.float32
        )
        score_grad_low = (
            probabilities * (prob_grad - jnp.sum(probabilities * prob_grad, axis=-1, keepdims=True))
        ).astype(jnp.bfloat16)
        query_grad = (
            jnp.einsum(
                "hgst,thd->shgd", score_grad_low, key_rows, preferred_element_type=jnp.float32
            )
            * score_scale
        )
        key_grad = (
            key_grad
            + jnp.einsum(
                "hgst,shgd->thd", score_grad_low, query_part, preferred_element_type=jnp.float32
            )
            * score_scale
        )
        return ((key_grad, value_grad), query_grad)

    offsets = jnp.arange(0, row_count, block_rows, dtype=jnp.int32)
    zeros_kv = jnp.zeros(key_rows.shape, jnp.float32)
    (key_grad, value_grad), query_grads = lax.scan(
        one_block, (zeros_kv, zeros_kv), (offsets, log_totals)
    )
    return (query_grads.reshape(queries.shape), key_grad, value_grad)


def tensor_sum(values):
    if lax.axis_size("tensor") != 2:
        return lax.psum(values, "tensor")
    swapped = lax.ppermute(values, "tensor", perm=[(0, 1), (1, 0)])
    return jax.tree.map(lambda mine, theirs: mine + theirs, values, swapped)


def dp_sum(row_split, col_split, vectors):
    n_dp = lax.axis_size("dp")
    pieces = [g.reshape(n_dp, -1) for g in row_split]
    pieces += [
        g.reshape(g.shape[0], n_dp, g.shape[1] // n_dp).transpose(1, 0, 2).reshape(n_dp, -1)
        for g in col_split
    ]
    pieces += [jnp.broadcast_to(v.reshape(1, -1), (n_dp, v.size)) for v in vectors]
    widths = [p.shape[1] for p in pieces]
    lane_rows = -(-sum(widths) // 16384) * 128
    pieces.append(jnp.zeros((n_dp, lane_rows * 128 - sum(widths)), jnp.float32))
    packed = lax.psum_scatter(
        jnp.concatenate(pieces, axis=1).reshape(n_dp * lane_rows, 128),
        "dp",
        scatter_dimension=0,
        tiled=True,
    ).reshape(-1)
    shapes = [(g.shape[0] // n_dp, g.shape[1]) for g in row_split]
    shapes += [(g.shape[0], g.shape[1] // n_dp) for g in col_split]
    shapes += [v.shape for v in vectors]
    outs = []
    at = 0
    for w, s in zip(widths, shapes):
        outs.append(packed[at : at + w].reshape(s))
        at += w
    return outs


def body(
    tokens,
    cotangent,
    lengths,
    norm_gain,
    query_weight,
    key_weight,
    value_weight,
    attn_out_weight,
    z_weight,
    x_weight,
    bc_weight,
    dt_weight,
    conv_x,
    conv_x_bias,
    conv_bc,
    conv_bc_bias,
    dt_bias,
    a_log,
    skip_gain,
    mixer_gain,
    mamba_out_weight,
    ffn_gain,
    gate_weight,
    up_weight,
    down_weight,
):
    position, owners, validity, carry_on = layout(lengths[0])
    row_count = tokens.shape[0]
    kv_local = key_weight.shape[1] // HEAD_DIM
    grouping = query_weight.shape[1] // key_weight.shape[1]
    group_width = SSM_HEADS * SSM_HEAD_DIM
    valid_col = validity[:, None]
    tokens_wide = tokens.astype(jnp.float32)
    normed, first_norm_back = jax.vjp(rms_norm, tokens_wide, norm_gain)
    first_in = normed.astype(jnp.bfloat16)
    rotation = partial(rotate, position=position)
    query_lin = project(first_in, query_weight).reshape(row_count, kv_local, grouping, HEAD_DIM)
    key_lin = project(first_in, key_weight).reshape(row_count, kv_local, HEAD_DIM)
    value_rows = (
        project(first_in, value_weight).reshape(row_count, kv_local, HEAD_DIM).astype(jnp.bfloat16)
    )
    query_turned, query_unturn = jax.vjp(rotation, query_lin)
    key_turned, key_unturn = jax.vjp(rotation, key_lin)
    queries = query_turned.astype(jnp.bfloat16)
    key_rows = key_turned.astype(jnp.bfloat16)
    attended_wide, log_totals = attend_forward(queries, key_rows, value_rows, owners)
    attended = attended_wide.reshape(row_count, -1).astype(jnp.bfloat16)
    gate_lin = project(first_in, z_weight)
    stream_lin = project(first_in, x_weight)
    bc_lin = project(first_in, bc_weight)
    step_lin = project(first_in, dt_weight)
    causal_filter = partial(convolve, position=position)
    streams_wide, stream_back = jax.vjp(
        causal_filter, stream_lin, conv_x.astype(jnp.float32), conv_x_bias.astype(jnp.float32)
    )
    bc_wide, bc_back = jax.vjp(
        causal_filter, bc_lin, conv_bc.astype(jnp.float32), conv_bc_bias.astype(jnp.float32)
    )
    streams = streams_wide.astype(jnp.bfloat16)
    bc_values = bc_wide.astype(jnp.bfloat16)
    ssm_core = partial(mamba_core, carry_on=carry_on)
    gated_wide, core_back = jax.vjp(
        ssm_core,
        streams.astype(jnp.float32),
        bc_values.astype(jnp.float32),
        gate_lin,
        step_lin,
        dt_bias,
        a_log,
        skip_gain,
    )
    square_sum = lax.psum(jnp.sum(gated_wide * gated_wide, axis=-1), "tensor")
    group_scale = lax.rsqrt(square_sum / group_width + EPSILON)[:, None]
    normed_gated = gated_wide * group_scale
    mixed = (normed_gated * mixer_gain[None, :]).astype(jnp.bfloat16)
    branch_part = project(attended, attn_out_weight) + project(mixed, mamba_out_weight)
    branch = tensor_sum(branch_part)
    middle = tokens_wide + valid_col * branch
    second_wide, second_norm_back = jax.vjp(rms_norm, middle, ffn_gain)
    second_in = second_wide.astype(jnp.bfloat16)
    gate_values = project(second_in, gate_weight)
    up_values = project(second_in, up_weight)
    hidden_wide, hidden_back = jax.vjp(swiglu, gate_values, up_values)
    hidden = hidden_wide.astype(jnp.bfloat16)
    ffn_full = tensor_sum(project(hidden, down_weight))
    cot_wide = cotangent.astype(jnp.float32)
    grad_ffn = (valid_col * cot_wide).astype(jnp.bfloat16)
    down_grad = outer_rows(hidden, grad_ffn)
    grad_hidden = back_project(grad_ffn, down_weight)
    grad_gate_wide, grad_up_wide = hidden_back(grad_hidden)
    grad_gate = grad_gate_wide.astype(jnp.bfloat16)
    grad_up = grad_up_wide.astype(jnp.bfloat16)
    gate_grad = outer_rows(second_in, grad_gate)
    up_grad = outer_rows(second_in, grad_up)
    grad_second = tensor_sum(
        back_project(grad_gate, gate_weight) + back_project(grad_up, up_weight),
    )
    grad_middle_norm, ffn_gain_grad = second_norm_back(grad_second)
    grad_middle = cot_wide + grad_middle_norm
    grad_branch = (valid_col * grad_middle).astype(jnp.bfloat16)
    attn_out_grad = outer_rows(attended, grad_branch)
    mamba_out_grad = outer_rows(mixed, grad_branch)
    grad_attended = (
        back_project(grad_branch, attn_out_weight)
        .astype(jnp.bfloat16)
        .reshape(row_count, kv_local, grouping, HEAD_DIM)
    )
    grad_mixed = back_project(grad_branch, mamba_out_weight)
    gain_scaled = grad_mixed * mixer_gain[None, :]
    mixer_gain_grad = jnp.sum(grad_mixed * normed_gated, axis=0)
    cross_sum = lax.psum(jnp.sum(gain_scaled * normed_gated, axis=-1), "tensor")
    grad_gated = group_scale * (gain_scaled - normed_gated * (cross_sum / group_width)[:, None])
    grad_streams, grad_bc, grad_gate_lin, grad_step_lin, dt_bias_grad, a_log_grad, skip_grad = (
        core_back(grad_gated)
    )
    grad_stream_lin, conv_x_grad, conv_x_bias_grad = stream_back(grad_streams)
    grad_bc_lin, conv_bc_part, conv_bc_bias_part = bc_back(grad_bc)
    grad_query, grad_key, grad_value = attend_backward(
        queries, key_rows, value_rows, owners, log_totals, grad_attended
    )
    (grad_query_lin,) = query_unturn(grad_query)
    (grad_key_lin,) = key_unturn(grad_key)
    grad_query_low = grad_query_lin.reshape(row_count, -1).astype(jnp.bfloat16)
    grad_key_low = grad_key_lin.reshape(row_count, -1).astype(jnp.bfloat16)
    grad_value_low = grad_value.reshape(row_count, -1).astype(jnp.bfloat16)
    grad_gate_low = grad_gate_lin.astype(jnp.bfloat16)
    grad_stream_low = grad_stream_lin.astype(jnp.bfloat16)
    grad_step_low = grad_step_lin.astype(jnp.bfloat16)
    query_grad = outer_rows(first_in, grad_query_low)
    key_grad = outer_rows(first_in, grad_key_low)
    value_grad = outer_rows(first_in, grad_value_low)
    z_grad = outer_rows(first_in, grad_gate_low)
    x_grad = outer_rows(first_in, grad_stream_low)
    dt_grad = outer_rows(first_in, grad_step_low)
    bc_part = lax.dot_general(
        first_in.astype(jnp.float32), grad_bc_lin, (((0,), (0,)), ((), ())), precision=PRECISE
    )
    grad_first_part = (
        back_project(grad_query_low, query_weight)
        + back_project(grad_key_low, key_weight)
        + back_project(grad_value_low, value_weight)
        + back_project(grad_gate_low, z_weight)
        + back_project(grad_stream_low, x_weight)
        + back_project(grad_step_low, dt_weight)
        + lax.dot_general(
            grad_bc_lin, bc_weight.astype(jnp.float32), (((1,), (1,)), ((), ())), precision=PRECISE
        )
    )
    first_scale = lax.rsqrt(jnp.mean(tokens_wide * tokens_wide, axis=-1, keepdims=True) + EPSILON)
    norm_gain_part = jnp.sum(grad_first_part * (tokens_wide * first_scale), axis=0)
    grad_first_part, norm_gain_part = lax.optimization_barrier((grad_first_part, norm_gain_part))
    grad_first = tensor_sum(grad_first_part)
    grad_tokens_norm, _ = first_norm_back(grad_first)
    ffn_late, middle_late, _ = lax.optimization_barrier((ffn_full, middle, grad_first))
    block_output = (middle_late + valid_col * ffn_late).astype(jnp.bfloat16)
    tokens_grad = (grad_middle + grad_tokens_norm).astype(jnp.bfloat16)
    early = dp_sum(
        (gate_grad, up_grad, query_grad, key_grad, value_grad),
        (attn_out_grad, mamba_out_grad, down_grad),
        (),
    )
    late = dp_sum(
        (z_grad, x_grad, bc_part, dt_grad),
        (),
        (
            norm_gain_part,
            conv_x_grad,
            conv_x_bias_grad,
            conv_bc_part,
            conv_bc_bias_part,
            dt_bias_grad,
            a_log_grad,
            skip_grad,
            mixer_gain_grad,
            ffn_gain_grad,
        ),
    )
    late = list(late)
    late[2], late[4], late[7], late[8] = tensor_sum((late[2], late[4], late[7], late[8]))
    matrix_sums = (
        early[2],
        early[3],
        early[4],
        early[5],
        late[0],
        late[1],
        late[2],
        late[3],
        early[6],
        early[0],
        early[1],
        early[7],
    )
    vector_sums = late[4:]
    return (
        block_output,
        tokens_grad,
        vector_sums[0],
        matrix_sums[0],
        matrix_sums[1],
        matrix_sums[2],
        matrix_sums[3],
        matrix_sums[4],
        matrix_sums[5],
        matrix_sums[6],
        matrix_sums[7],
        vector_sums[1],
        vector_sums[2],
        vector_sums[3],
        vector_sums[4],
        vector_sums[5],
        vector_sums[6],
        vector_sums[7],
        vector_sums[8],
        matrix_sums[8],
        vector_sums[9],
        matrix_sums[9],
        matrix_sums[10],
        matrix_sums[11],
    )


def solution(mesh):
    return jax.shard_map(
        body,
        mesh=mesh,
        in_specs=(
            P("dp", None),
            P("dp", None),
            P("dp", None),
            P(),
            P(None, "tensor"),
            P(None, "tensor"),
            P(None, "tensor"),
            P("tensor", None),
            P(None, "tensor"),
            P(None, "tensor"),
            P(),
            P(None, "tensor"),
            P(None, "tensor"),
            P("tensor"),
            P(),
            P(),
            P("tensor"),
            P("tensor"),
            P("tensor"),
            P("tensor"),
            P("tensor", None),
            P(),
            P(None, "tensor"),
            P(None, "tensor"),
            P("tensor", None),
        ),
        out_specs=(
            P("dp", None),
            P("dp", None),
            P(),
            P("dp", "tensor"),
            P("dp", "tensor"),
            P("dp", "tensor"),
            P("tensor", "dp"),
            P("dp", "tensor"),
            P("dp", "tensor"),
            P("dp", None),
            P("dp", "tensor"),
            P(None, "tensor"),
            P("tensor"),
            P(),
            P(),
            P("tensor"),
            P("tensor"),
            P("tensor"),
            P("tensor"),
            P("tensor", "dp"),
            P(),
            P("dp", "tensor"),
            P("dp", "tensor"),
            P("tensor", "dp"),
        ),
        check_vma=False,
    )
```
